256 devices in a mesh: dp: 8 (over z), ctx: 32 (over y, x, core).
Axes of the slice: x: 4, y: 4, z: 8, core: 2. Of those that a mesh axis runs over, the one named last changes fastest.
Arguments:
- queries: bfloat16 [32768, 4096], P(('dp', 'ctx')), parts along dimension 0, may hold values from -0.6640625 to 0.6640625
- key_vectors: bfloat16 [32768, 4096], P(('dp', 'ctx')), parts along dimension 0, may hold values from -0.6640625 to 0.6640625
- values: bfloat16 [32768, 4096], P(('dp', 'ctx')), parts along dimension 0, may hold values from -0.6640625 to 0.6640625
- out_grad: bfloat16 [32768, 4096], P(('dp', 'ctx')), parts along dimension 0, may hold values from -0.6640625 to 0.6640625
- log_decay: bfloat16 [32768, 32], P(('dp', 'ctx')), parts along dimension 0, may hold values from -2.2 to 0
Outputs:
- attended: bfloat16 [32768, 4096], P(('dp', 'ctx')), parts along dimension 0
- query_grad: bfloat16 [32768, 4096], P(('dp', 'ctx')), parts along dimension 0
- key_grad: bfloat16 [32768, 4096], P(('dp', 'ctx')), parts along dimension 0
- value_grad: bfloat16 [32768, 4096], P(('dp', 'ctx')), parts along dimension 0
The draws below stay inside these ranges and needn't reach their ends.
There are 8 independent parts, one for each index of `dp`. The reference program is written for one: setup_inputs(seed, part) draws one part's arguments, and reference() takes and returns one part's arrays. A program takes and returns all parts, laid end to end along the dimension named above; each array names one. Nothing has to cross between parts.
All inputs are finite; a program needn't handle non-finite values.
Results may differ from the reference program's by a relative error of at most 0.001.
Values may be sent and summed in bfloat16 or wider, within the bound.
No kernel may reach another device: no remote copies, remote signals or barrier semaphores. Data moves between devices by JAX's collectives and lax.ppermute only.
A program may use at most 320 MiB of HBM per device.

```python
import math
import jax
import jax.numpy as jnp
from jax import lax

HEAD_COUNT_HALF = 32
DK = 128
SPAN = 64
TOK_DEV = 128
TOKEN_LENGTH = 4096


def draw_log_decay(key, part):
    key_rows_full = jax.random.split(key, 8)
    keep_share = 5
    slow_heads = jax.random.randint(key_rows_full[0], (HEAD_COUNT_HALF,), 0, 10) < keep_share
    fast_rate = jnp.exp(jax.random.uniform(key_rows_full[1], (HEAD_COUNT_HALF,), jnp.float32, math.log(1.0 / 50.0), math.log(1.0 / 30.0)))
    slow_rate = jnp.exp(jax.random.uniform(key_rows_full[2], (HEAD_COUNT_HALF,), jnp.float32, math.log(0.02 / TOKEN_LENGTH), math.log(0.5 / TOKEN_LENGTH)))
    per_head_rate = jnp.where(slow_heads, slow_rate, fast_rate)
    random_noise = jax.random.uniform(key_rows_full[3], (TOKEN_LENGTH, HEAD_COUNT_HALF), jnp.float32, 0.5, 2.0)
    token_positions = jnp.arange(TOKEN_LENGTH)
    segment_shift = jax.random.randint(key_rows_full[6], (), 0, TOK_DEV)
    segment_index = (token_positions + segment_shift) // TOK_DEV
    segment_count = TOKEN_LENGTH // TOK_DEV + 1
    segment_scale = jnp.exp(jax.random.uniform(key_rows_full[7], (segment_count, HEAD_COUNT_HALF), jnp.float32, math.log(0.01), 0.0))
    segment_factor = segment_scale[segment_index]
    spike_locations = jax.random.randint(key_rows_full[4], (3,), 0, TOKEN_LENGTH)
    spike_depth = jax.random.uniform(key_rows_full[5], (3, HEAD_COUNT_HALF), jnp.float32, math.log(0.5), math.log(0.8))
    spike_hits = (token_positions[None, :, None] == spike_locations[:, None, None]).astype(jnp.float32)
    spike_events = jnp.sum(spike_hits * spike_depth[:, None, :], axis=0)
    return (-per_head_rate[None, :] * random_noise * segment_factor + spike_events).astype(jnp.bfloat16)


def levels(key, dims, cuts, low, top_value):
    def one(dim, blocks):
        draws = jax.random.uniform(jax.random.fold_in(jax.random.fold_in(key, 6), dim), (blocks,), jnp.float32, low / len(cuts), top_value / len(cuts))
        return jnp.repeat(jnp.exp(draws), dims[dim] // blocks).reshape((-1,) + (1,) * (len(dims) - dim - 1))

    level = one(*cuts[0])
    for cut in cuts[1:]:
        level = level * one(*cut)
    return level


def centred(key, shape, scale, most, cuts=(), kind=jnp.bfloat16):
    values = jax.random.normal(key, shape, jnp.float32) * scale
    if len(cuts) > 0:
        values = levels(key, shape, cuts, -0.22, 0.18) * values
    return jnp.clip(values, min=-most, max=most).astype(kind)


def setup_inputs(seed: int = 0, part: int = 0) -> dict:
    arg_keys = jax.random.split(jax.random.key(seed), 6)
    part_splits = jax.random.split(jax.random.fold_in(arg_keys[5], part), 6)
    queries = centred(part_splits[0], (TOKEN_LENGTH, HEAD_COUNT_HALF * DK), 0.111, 0.6640625, ((0, 32),))
    key_vectors = centred(part_splits[1], (TOKEN_LENGTH, HEAD_COUNT_HALF * DK), 0.111, 0.6640625, ((0, 32),))
    values = centred(part_splits[2], (TOKEN_LENGTH, HEAD_COUNT_HALF * DK), 0.111, 0.6640625, ((0, 32),))
    out_grad = centred(part_splits[3], (TOKEN_LENGTH, HEAD_COUNT_HALF * DK), 0.111, 0.6640625, ((0, 32),))
    log_decay = draw_log_decay(jax.random.fold_in(jax.random.fold_in(arg_keys[5], part), 71), part)
    return {"queries": queries, "key_vectors": key_vectors, "values": values, "out_grad": out_grad, "log_decay": log_decay}


def combine(earlier, latter):
    return (earlier[0] + latter[0], jnp.exp(latter[0])[..., None, None] * earlier[1] + latter[1])


def head_pass(queries, key_vectors, values, out_grad, log_decay, state_in, grad_in):
    highest = lax.Precision.HIGHEST
    blocks = queries.shape[0] // SPAN
    q_rows = queries.reshape(blocks, SPAN, -1)
    k_rows = key_vectors.reshape(blocks, SPAN, -1)
    v_rows = values.reshape(blocks, SPAN, -1)
    g_rows = out_grad.reshape(blocks, SPAN, -1)
    cumul = jnp.cumsum(log_decay.reshape(blocks, SPAN), axis=1)
    totals = cumul[:, -1]
    causal = jnp.tril(jnp.ones((SPAN, SPAN), dtype=bool))
    spread = cumul[:, :, None] - cumul[:, None, :]
    weights = jnp.where(causal, jnp.exp(jnp.where(causal, spread, 0.0)), 0.0)
    scores = jnp.einsum("nte,nse->nts", q_rows, k_rows, precision=highest) * weights
    grad_scores = jnp.einsum("nte,nse->nts", g_rows, v_rows, precision=highest) * weights
    key_decay = jnp.exp(totals[:, None] - cumul)[:, :, None]
    query_decay = jnp.exp(cumul)[:, :, None]
    q_scaled = q_rows * query_decay
    g_scaled = g_rows * query_decay
    k_scaled = k_rows * key_decay
    v_scaled = v_rows * key_decay
    updates = jnp.einsum("nse,nsf->nef", k_scaled, v_rows, precision=highest)
    grad_states = jnp.einsum("nte,ntf->nef", q_scaled, g_rows, precision=highest)
    anchor = jnp.zeros((1,), jnp.float32)
    forward = lax.associative_scan(combine, (jnp.concatenate([anchor, totals]), jnp.concatenate([state_in[None], updates])))
    starts = forward[1][:blocks]
    backward = lax.associative_scan(combine, (jnp.concatenate([anchor, totals[::-1]]), jnp.concatenate([grad_in[None], grad_states[::-1]])))
    after_grad = backward[1][:blocks][::-1]
    attended = jnp.einsum("nte,nef->ntf", q_scaled, starts, precision=highest) + jnp.einsum("nts,nsf->ntf", scores, v_rows, precision=highest)
    query_grad = jnp.einsum("ntf,nef->nte", g_scaled, starts, precision=highest) + jnp.einsum("nts,nse->nte", grad_scores, k_rows, precision=highest)
    key_grad = jnp.einsum("nsf,nef->nse", v_scaled, after_grad, precision=highest) + jnp.einsum("nts,nte->nse", grad_scores, q_rows, precision=highest)
    value_grad = jnp.einsum("nse,nef->nsf", k_scaled, after_grad, precision=highest) + jnp.einsum("nts,ntf->nsf", scores, g_rows, precision=highest)
    length = queries.shape[0]
    return (attended.reshape(length, -1), query_grad.reshape(length, -1), key_grad.reshape(length, -1), value_grad.reshape(length, -1))


def split_heads(matrix, head_count):
    return jnp.transpose(matrix.reshape(matrix.shape[0], head_count, -1), (1, 0, 2)).astype(jnp.float32)


def join_heads(stacked):
    return jnp.transpose(stacked, (1, 0, 2)).reshape(stacked.shape[1], -1).astype(jnp.bfloat16)


def run_head(pieces):
    return head_pass(*pieces)


def reference(queries, key_vectors, values, out_grad, log_decay):
    empty_state = jnp.zeros((HEAD_COUNT_HALF, DK, DK), jnp.float32)
    decays = jnp.transpose(log_decay).astype(jnp.float32)
    results = lax.map(run_head, (split_heads(queries, HEAD_COUNT_HALF), split_heads(key_vectors, HEAD_COUNT_HALF), split_heads(values, HEAD_COUNT_HALF), split_heads(out_grad, HEAD_COUNT_HALF), decays, empty_state, empty_state))
    return (join_heads(results[0]), join_heads(results[1]), join_heads(results[2]), join_heads(results[3]))
```

```python
import jax
import jax.numpy as jnp
from jax import lax
from jax.sharding import PartitionSpec as P

SPAN = 64


def combine(earlier, latter):
    return (earlier[0] + latter[0], jnp.exp(latter[0])[..., None, None] * earlier[1] + latter[1])


def prepare(queries, key_vectors, values, out_grad, log_decay):
    highest = lax.Precision.HIGHEST
    length = queries.shape[0]
    heads = log_decay.shape[1]
    blocks = length // SPAN
    q_rows = queries.reshape(blocks, SPAN, heads, -1)
    k_rows = key_vectors.reshape(blocks, SPAN, heads, -1)
    v_rows = values.reshape(blocks, SPAN, heads, -1)
    g_rows = out_grad.reshape(blocks, SPAN, heads, -1)
    cumul = jnp.cumsum(log_decay.astype(jnp.float32).reshape(blocks, SPAN, heads), axis=1)
    totals = cumul[:, -1, :]
    causal = jnp.tril(jnp.ones((SPAN, SPAN), dtype=bool))
    head_cumul = jnp.transpose(cumul, (0, 2, 1))
    spread = head_cumul[:, :, :, None] - head_cumul[:, :, None, :]
    weights = jnp.where(causal, jnp.exp(jnp.where(causal, spread, 0.0)), 0.0)
    scores = (
        jnp.einsum("bthe,bshe->bhts", q_rows, k_rows, preferred_element_type=jnp.float32) * weights
    )
    grad_scores = (
        jnp.einsum("bthe,bshe->bhts", g_rows, v_rows, preferred_element_type=jnp.float32) * weights
    )
    query_decay = jnp.exp(cumul)[..., None]
    key_decay = jnp.exp(totals[:, None, :] - cumul)[..., None]
    q_scaled = q_rows.astype(jnp.float32) * query_decay
    g_scaled = g_rows.astype(jnp.float32) * query_decay
    k_scaled = k_rows.astype(jnp.float32) * key_decay
    v_scaled = v_rows.astype(jnp.float32) * key_decay
    updates = jnp.einsum("bshe,bshf->bhef", k_scaled, v_rows.astype(jnp.float32), precision=highest)
    grad_states = jnp.einsum(
        "bthe,bthf->bhef", q_scaled, g_rows.astype(jnp.float32), precision=highest
    )
    forward = lax.associative_scan(combine, (totals, updates))
    backward = lax.associative_scan(combine, (totals, grad_states), reverse=True)
    zero_block = jnp.zeros_like(updates[:1])
    local_starts = jnp.concatenate([zero_block, forward[1][:-1]], axis=0)
    local_after = jnp.concatenate([backward[1][1:], zero_block], axis=0)
    running = jnp.cumsum(totals, axis=0)
    before_decay = jnp.exp(running - totals)
    after_decay = jnp.exp(running[-1][None, :] - running)
    pieces = (
        q_rows,
        k_rows,
        v_rows,
        g_rows,
        scores,
        grad_scores,
        q_scaled,
        g_scaled,
        k_scaled,
        v_scaled,
        local_starts,
        local_after,
        before_decay,
        after_decay,
    )
    return (running[-1], forward[1][-1], backward[1][0], pieces)


def finish(pieces, state_in, grad_in):
    highest = lax.Precision.HIGHEST
    (
        q_rows,
        k_rows,
        v_rows,
        g_rows,
        scores,
        grad_scores,
        q_scaled,
        g_scaled,
        k_scaled,
        v_scaled,
        local_starts,
        local_after,
        before_decay,
        after_decay,
    ) = pieces
    starts = local_starts + before_decay[:, :, None, None] * state_in[None]
    after_grad = local_after + after_decay[:, :, None, None] * grad_in[None]
    attended = jnp.einsum("bthe,bhef->bthf", q_scaled, starts, precision=highest) + jnp.einsum(
        "bhts,bshf->bthf", scores, v_rows.astype(jnp.float32), precision=highest
    )
    query_grad = jnp.einsum("bthf,bhef->bthe", g_scaled, starts, precision=highest) + jnp.einsum(
        "bhts,bshe->bthe", grad_scores, k_rows.astype(jnp.float32), precision=highest
    )
    key_grad = jnp.einsum("bshf,bhef->bshe", v_scaled, after_grad, precision=highest) + jnp.einsum(
        "bhts,bthe->bshe", grad_scores, q_rows.astype(jnp.float32), precision=highest
    )
    value_grad = jnp.einsum(
        "bshe,bhef->bshf", k_scaled, after_grad, precision=highest
    ) + jnp.einsum("bhts,bthf->bshf", scores, g_rows.astype(jnp.float32), precision=highest)
    length = q_rows.shape[0] * q_rows.shape[1]
    return tuple(
        (
            result.reshape(length, -1).astype(jnp.bfloat16)
            for result in (attended, query_grad, key_grad, value_grad)
        )
    )


def chip_scan(total, state, axis, chips, reverse):
    direction = -1 if reverse else 1
    def shifted(pair, step):
        pairs = []
        for chip in range(chips):
            target = chip + direction * step
            if 0 <= target < chips:
                for core in range(2):
                    pairs.append((2 * chip + core, 2 * target + core))
        return jax.tree.map(lambda a: lax.ppermute(a, axis, pairs), pair)

    current = shifted((total, state), 1)
    step = 1
    while step < chips:
        received = shifted(current, step)
        current = combine(received, current)
        step *= 2
    return current


def shards(queries, key_vectors, values, out_grad, log_decay):
    axis = "ctx"
    total, state, grad_state, pieces = prepare(queries, key_vectors, values, out_grad, log_decay)
    heads = total.shape[0]
    half = heads // 2
    chips = lax.axis_size(axis) // 2
    core = lax.axis_index(axis) % 2
    partner = [(2 * c + k, 2 * c + 1 - k) for c in range(chips) for k in range(2)]

    def other_half(a):
        return lax.dynamic_slice_in_dim(a, (1 - core) * half, half, 0)

    def own_half(a):
        return lax.dynamic_slice_in_dim(a, core * half, half, 0)

    sent = (total, other_half(state), other_half(grad_state))
    other_total, other_state, other_grad = lax.ppermute(sent, axis, partner)
    first = core == 0
    mine_state = own_half(state)
    mine_grad = own_half(grad_state)
    own_total_half = own_half(total)
    other_total_half = own_half(other_total)
    one = jnp.ones_like(own_total_half)
    fwd_a = jnp.where(first, jnp.exp(other_total_half), one)[:, None, None]
    fwd_b = jnp.where(first, one, jnp.exp(own_total_half))[:, None, None]
    chip_state = fwd_a * mine_state + fwd_b * other_state
    bwd_a = jnp.where(first, one, jnp.exp(other_total_half))[:, None, None]
    bwd_b = jnp.where(first, jnp.exp(own_total_half), one)[:, None, None]
    chip_grad = bwd_a * mine_grad + bwd_b * other_grad
    chip_total = own_half(total + other_total)
    before = chip_scan(chip_total, chip_state, axis, chips, False)[1]
    after = chip_scan(chip_total, chip_grad, axis, chips, True)[1]
    total_c0 = jnp.where(first, own_total_half, other_total_half)
    total_c1 = jnp.where(first, other_total_half, own_total_half)
    state_c0 = jnp.where(first, mine_state, other_state)
    grad_c1 = jnp.where(first, other_grad, mine_grad)
    fwd_core0 = before
    fwd_core1 = jnp.exp(total_c0)[:, None, None] * before + state_c0
    bwd_core0 = jnp.exp(total_c1)[:, None, None] * after + grad_c1
    bwd_core1 = after
    keep_fwd = jnp.where(first, fwd_core0, fwd_core1)
    keep_bwd = jnp.where(first, bwd_core0, bwd_core1)
    give_fwd = jnp.where(first, fwd_core1, fwd_core0)
    give_bwd = jnp.where(first, bwd_core1, bwd_core0)
    got_fwd, got_bwd = lax.ppermute((give_fwd, give_bwd), axis, partner)

    def assemble(keep, got):
        return jnp.where(first, jnp.concatenate([keep, got], 0), jnp.concatenate([got, keep], 0))

    return finish(pieces, assemble(keep_fwd, got_fwd), assemble(keep_bwd, got_bwd))


def solution(mesh):
    return jax.shard_map(
        shards,
        mesh=mesh,
        in_specs=(
            P(("dp", "ctx"), None),
            P(("dp", "ctx"), None),
            P(("dp", "ctx"), None),
            P(("dp", "ctx"), None),
            P(("dp", "ctx"), None),
        ),
        out_specs=(
            P(("dp", "ctx"), None),
            P(("dp", "ctx"), None),
            P(("dp", "ctx"), None),
            P(("dp", "ctx"), None),
        ),
        check_vma=False,
    )
```

```python
import jax
import jax.numpy as jnp
from jax import lax
from jax.sharding import PartitionSpec as P

SPAN = 64


def combine(earlier, latter):
    return (earlier[0] + latter[0], jnp.exp(latter[0])[..., None, None] * earlier[1] + latter[1])


def prepare(queries, key_vectors, values, out_grad, log_decay):
    highest = lax.Precision.HIGHEST
    length = queries.shape[0]
    heads = log_decay.shape[1]
    blocks = length // SPAN
    q_rows = queries.reshape(blocks, SPAN, heads, -1)
    k_rows = key_vectors.reshape(blocks, SPAN, heads, -1)
    v_rows = values.reshape(blocks, SPAN, heads, -1)
    g_rows = out_grad.reshape(blocks, SPAN, heads, -1)
    cumul = jnp.cumsum(log_decay.astype(jnp.float32).reshape(blocks, SPAN, heads), axis=1)
    totals = cumul[:, -1, :]
    causal = jnp.tril(jnp.ones((SPAN, SPAN), dtype=bool))
    head_cumul = jnp.transpose(cumul, (0, 2, 1))
    spread = head_cumul[:, :, :, None] - head_cumul[:, :, None, :]
    weights = jnp.where(causal, jnp.exp(jnp.where(causal, spread, 0.0)), 0.0)
    scores = (
        jnp.einsum("bthe,bshe->bhts", q_rows, k_rows, preferred_element_type=jnp.float32) * weights
    )
    grad_scores = (
        jnp.einsum("bthe,bshe->bhts", g_rows, v_rows, preferred_element_type=jnp.float32) * weights
    )
    query_decay = jnp.exp(cumul)[..., None]
    key_decay = jnp.exp(totals[:, None, :] - cumul)[..., None]
    q_scaled = q_rows.astype(jnp.float32) * query_decay
    g_scaled = g_rows.astype(jnp.float32) * query_decay
    k_scaled = k_rows.astype(jnp.float32) * key_decay
    v_scaled = v_rows.astype(jnp.float32) * key_decay
    updates = jnp.einsum("bshe,bshf->bhef", k_scaled, v_rows.astype(jnp.float32), precision=highest)
    grad_states = jnp.einsum(
        "bthe,bthf->bhef", q_scaled, g_rows.astype(jnp.float32), precision=highest
    )
    forward = lax.associative_scan(combine, (totals, updates))
    backward = lax.associative_scan(combine, (totals, grad_states), reverse=True)
    zero_block = jnp.zeros_like(updates[:1])
    local_starts = jnp.concatenate([zero_block, forward[1][:-1]], axis=0)
    local_after = jnp.concatenate([backward[1][1:], zero_block], axis=0)
    running = jnp.cumsum(totals, axis=0)
    before_decay = jnp.exp(running - totals)
    after_decay = jnp.exp(running[-1][None, :] - running)
    pieces = (
        q_rows,
        k_rows,
        v_rows,
        g_rows,
        scores,
        grad_scores,
        q_scaled,
        g_scaled,
        k_scaled,
        v_scaled,
        local_starts,
        local_after,
        before_decay,
        after_decay,
    )
    return (running[-1], forward[1][-1], backward[1][0], pieces)


def finish(pieces, state_in, grad_in):
    highest = lax.Precision.HIGHEST
    (
        q_rows,
        k_rows,
        v_rows,
        g_rows,
        scores,
        grad_scores,
        q_scaled,
        g_scaled,
        k_scaled,
        v_scaled,
        local_starts,
        local_after,
        before_decay,
        after_decay,
    ) = pieces
    starts = local_starts + before_decay[:, :, None, None] * state_in[None]
    after_grad = local_after + after_decay[:, :, None, None] * grad_in[None]
    attended = jnp.einsum("bthe,bhef->bthf", q_scaled, starts, precision=highest) + jnp.einsum(
        "bhts,bshf->bthf", scores, v_rows.astype(jnp.float32), precision=highest
    )
    query_grad = jnp.einsum("bthf,bhef->bthe", g_scaled, starts, precision=highest) + jnp.einsum(
        "bhts,bshe->bthe", grad_scores, k_rows.astype(jnp.float32), precision=highest
    )
    key_grad = jnp.einsum("bshf,bhef->bshe", v_scaled, after_grad, precision=highest) + jnp.einsum(
        "bhts,bthe->bshe", grad_scores, q_rows.astype(jnp.float32), precision=highest
    )
    value_grad = jnp.einsum(
        "bshe,bhef->bshf", k_scaled, after_grad, precision=highest
    ) + jnp.einsum("bhts,bthf->bshf", scores, g_rows.astype(jnp.float32), precision=highest)
    length = q_rows.shape[0] * q_rows.shape[1]
    return tuple(
        (
            result.reshape(length, -1).astype(jnp.bfloat16)
            for result in (attended, query_grad, key_grad, value_grad)
        )
    )


def window_sum(ordered, place, first, last):
    total = jnp.zeros_like(ordered[0])
    for back in range(first, last + 1):
        index = place - back
        picked = lax.dynamic_index_in_dim(ordered, jnp.maximum(index, 0), 0, False)
        total = total + jnp.where(index >= 0, picked, jnp.zeros_like(picked))
    return total


def chip_scan(chip_totals, state, axis, chip, chips, reverse, steps):
    direction = -1 if reverse else 1
    ordered = chip_totals[::-1] if reverse else chip_totals
    place = chips - 1 - chip if reverse else chip
    sent = state
    carried = jnp.zeros_like(state)
    for count, step in enumerate(steps):
        pairs = []
        for c in range(chips):
            target = c + direction * step
            if 0 <= target < chips:
                for core in range(2):
                    pairs.append((2 * c + core, 2 * target + core))
        received = lax.ppermute(sent, axis, pairs)
        to_start = jnp.exp(window_sum(ordered, place, 1, step - 1))[:, None, None]
        carried = carried + to_start * received
        if count + 1 < len(steps):
            to_end = jnp.exp(window_sum(ordered, place, 0, step - 1))[:, None, None]
            sent = sent + to_end * received
    return carried


def shards(queries, key_vectors, values, out_grad, log_decay):
    axis = "ctx"
    total, state, grad_state, pieces = prepare(queries, key_vectors, values, out_grad, log_decay)
    heads = total.shape[0]
    half = heads // 2
    chips = lax.axis_size(axis) // 2
    core = lax.axis_index(axis) % 2
    partner = [(2 * c + k, 2 * c + 1 - k) for c in range(chips) for k in range(2)]

    def other_half(a):
        return lax.dynamic_slice_in_dim(a, (1 - core) * half, half, 0)

    def own_half(a):
        return lax.dynamic_slice_in_dim(a, core * half, half, 0)

    sent = (total, other_half(state), other_half(grad_state))
    other_total, other_state, other_grad = lax.ppermute(sent, axis, partner)
    first = core == 0
    mine_state = own_half(state)
    mine_grad = own_half(grad_state)
    own_total_half = own_half(total)
    other_total_half = own_half(other_total)
    one = jnp.ones_like(own_total_half)
    fwd_a = jnp.where(first, jnp.exp(other_total_half), one)[:, None, None]
    fwd_b = jnp.where(first, one, jnp.exp(own_total_half))[:, None, None]
    chip_state = fwd_a * mine_state + fwd_b * other_state
    bwd_a = jnp.where(first, one, jnp.exp(other_total_half))[:, None, None]
    bwd_b = jnp.where(first, jnp.exp(own_total_half), one)[:, None, None]
    chip_grad = bwd_a * mine_grad + bwd_b * other_grad
    every_total = lax.all_gather(total, axis)
    chip_totals = every_total[0::2] + every_total[1::2]
    chip = lax.axis_index(axis) // 2
    steps = []
    step = 1
    while step < chips:
        steps.append(step)
        step *= 2
    turn = len(steps) // 2
    orders = (steps, steps[turn:] + steps[:turn])
    group = half // 2
    scans = []
    for chip_sum, reverse in ((chip_state, False), (chip_grad, True)):
        parts = []
        for g, order in enumerate(orders):
            group_totals = lax.dynamic_slice_in_dim(chip_totals, core * half + g * group, group, 1)
            parts.append(
                chip_scan(group_totals, chip_sum[g * group:(g + 1) * group], axis, chip, chips, reverse, order)
            )
        scans.append(jnp.concatenate(parts, 0))
    before, after = scans
    total_c0 = jnp.where(first, own_total_half, other_total_half)
    total_c1 = jnp.where(first, other_total_half, own_total_half)
    state_c0 = jnp.where(first, mine_state, other_state)
    grad_c1 = jnp.where(first, other_grad, mine_grad)
    fwd_core0 = before
    fwd_core1 = jnp.exp(total_c0)[:, None, None] * before + state_c0
    bwd_core0 = jnp.exp(total_c1)[:, None, None] * after + grad_c1
    bwd_core1 = after
    keep_fwd = jnp.where(first, fwd_core0, fwd_core1)
    keep_bwd = jnp.where(first, bwd_core0, bwd_core1)
    give_fwd = jnp.where(first, fwd_core1, fwd_core0)
    give_bwd = jnp.where(first, bwd_core1, bwd_core0)
    got_fwd, got_bwd = lax.ppermute((give_fwd, give_bwd), axis, partner)

    def assemble(keep, got):
        return jnp.where(first, jnp.concatenate([keep, got], 0), jnp.concatenate([got, keep], 0))

    return finish(pieces, assemble(keep_fwd, got_fwd), assemble(keep_bwd, got_bwd))


def solution(mesh):
    return jax.shard_map(
        shards,
        mesh=mesh,
        in_specs=(
            P(("dp", "ctx"), None),
            P(("dp", "ctx"), None),
            P(("dp", "ctx"), None),
            P(("dp", "ctx"), None),
            P(("dp", "ctx"), None),
        ),
        out_specs=(
            P(("dp", "ctx"), None),
            P(("dp", "ctx"), None),
            P(("dp", "ctx"), None),
            P(("dp", "ctx"), None),
        ),
        check_vma=False,
    )
```

```python
import jax
import jax.numpy as jnp
from jax import lax
from jax.sharding import PartitionSpec as P

SPAN = 64


def combine(earlier, latter):
    return (earlier[0] + latter[0], jnp.exp(latter[0])[..., None, None] * earlier[1] + latter[1])


def prepare(queries, key_vectors, values, out_grad, log_decay):
    highest = lax.Precision.HIGHEST
    length = queries.shape[0]
    heads = log_decay.shape[1]
    blocks = length // SPAN
    q_rows = queries.reshape(blocks, SPAN, heads, -1)
    k_rows = key_vectors.reshape(blocks, SPAN, heads, -1)
    v_rows = values.reshape(blocks, SPAN, heads, -1)
    g_rows = out_grad.reshape(blocks, SPAN, heads, -1)
    cumul = jnp.cumsum(log_decay.astype(jnp.float32).reshape(blocks, SPAN, heads), axis=1)
    totals = cumul[:, -1, :]
    causal = jnp.tril(jnp.ones((SPAN, SPAN), dtype=bool))
    head_cumul = jnp.transpose(cumul, (0, 2, 1))
    spread = head_cumul[:, :, :, None] - head_cumul[:, :, None, :]
    weights = jnp.where(causal, jnp.exp(jnp.where(causal, spread, 0.0)), 0.0)
    scores = (
        jnp.einsum("bthe,bshe->bhts", q_rows, k_rows, preferred_element_type=jnp.float32) * weights
    )
    grad_scores = (
        jnp.einsum("bthe,bshe->bhts", g_rows, v_rows, preferred_element_type=jnp.float32) * weights
    )
    query_decay = jnp.exp(cumul)[..., None]
    key_decay = jnp.exp(totals[:, None, :] - cumul)[..., None]
    q_scaled = q_rows.astype(jnp.float32) * query_decay
    g_scaled = g_rows.astype(jnp.float32) * query_decay
    k_scaled = k_rows.astype(jnp.float32) * key_decay
    v_scaled = v_rows.astype(jnp.float32) * key_decay
    updates = jnp.einsum("bshe,bshf->bhef", k_scaled, v_rows.astype(jnp.float32), precision=highest)
    grad_states = jnp.einsum(
        "bthe,bthf->bhef", q_scaled, g_rows.astype(jnp.float32), precision=highest
    )
    forward = lax.associative_scan(combine, (totals, updates))
    backward = lax.associative_scan(combine, (totals, grad_states), reverse=True)
    zero_block = jnp.zeros_like(updates[:1])
    local_starts = jnp.concatenate([zero_block, forward[1][:-1]], axis=0)
    local_after = jnp.concatenate([backward[1][1:], zero_block], axis=0)
    running = jnp.cumsum(totals, axis=0)
    before_decay = jnp.exp(running - totals)
    after_decay = jnp.exp(running[-1][None, :] - running)
    pieces = (
        q_rows,
        k_rows,
        v_rows,
        g_rows,
        scores,
        grad_scores,
        q_scaled,
        g_scaled,
        k_scaled,
        v_scaled,
        local_starts,
        local_after,
        before_decay,
        after_decay,
    )
    return (running[-1], forward[1][-1], backward[1][0], pieces)


def finish(pieces, state_in, grad_in):
    highest = lax.Precision.HIGHEST
    (
        q_rows,
        k_rows,
        v_rows,
        g_rows,
        scores,
        grad_scores,
        q_scaled,
        g_scaled,
        k_scaled,
        v_scaled,
        local_starts,
        local_after,
        before_decay,
        after_decay,
    ) = pieces
    attended = jnp.einsum("bthe,bhef->bthf", q_scaled, local_starts, precision=highest) + jnp.einsum(
        "bhts,bshf->bthf", scores, v_rows.astype(jnp.float32), precision=highest
    )
    query_grad = jnp.einsum("bthf,bhef->bthe", g_scaled, local_starts, precision=highest) + jnp.einsum(
        "bhts,bshe->bthe", grad_scores, k_rows.astype(jnp.float32), precision=highest
    )
    key_grad = jnp.einsum("bshf,bhef->bshe", v_scaled, local_after, precision=highest) + jnp.einsum(
        "bhts,bthe->bshe", grad_scores, q_rows.astype(jnp.float32), precision=highest
    )
    value_grad = jnp.einsum(
        "bshe,bhef->bshf", k_scaled, local_after, precision=highest
    ) + jnp.einsum("bhts,bthf->bshf", scores, g_rows.astype(jnp.float32), precision=highest)
    before = before_decay[:, None, :, None]
    after = after_decay[:, None, :, None]
    attended = attended + jnp.einsum("bthe,hef->bthf", q_scaled * before, state_in, precision=highest)
    query_grad = query_grad + jnp.einsum("bthf,hef->bthe", g_scaled * before, state_in, precision=highest)
    key_grad = key_grad + jnp.einsum("bshf,hef->bshe", v_scaled * after, grad_in, precision=highest)
    value_grad = value_grad + jnp.einsum("bshe,hef->bshf", k_scaled * after, grad_in, precision=highest)
    length = q_rows.shape[0] * q_rows.shape[1]
    return tuple(
        (
            result.reshape(length, -1).astype(jnp.bfloat16)
            for result in (attended, query_grad, key_grad, value_grad)
        )
    )


def gather_rows(row, axis):
    count = lax.axis_size(axis)
    me = lax.axis_index(axis)
    known = row[None]
    step = 1
    while step < count:
        pairs = [(i, (i + step) % count) for i in range(count)]
        known = jnp.concatenate([known, lax.ppermute(known, axis, pairs)], 0)
        step *= 2
    return known[(me - jnp.arange(count)) % count]


def window_sum(ordered, place, first, last):
    total = jnp.zeros_like(ordered[0])
    for back in range(first, last + 1):
        index = place - back
        picked = lax.dynamic_index_in_dim(ordered, jnp.maximum(index, 0), 0, False)
        total = total + jnp.where(index >= 0, picked, jnp.zeros_like(picked))
    return total


def chip_scan(chip_totals, state, axis, chip, chips, reverse, steps):
    direction = -1 if reverse else 1
    ordered = chip_totals[::-1] if reverse else chip_totals
    place = chips - 1 - chip if reverse else chip
    sent = state
    carried = jnp.zeros_like(state)
    for count, step in enumerate(steps):
        pairs = []
        for c in range(chips):
            target = c + direction * step
            if 0 <= target < chips:
                for core in range(2):
                    pairs.append((2 * c + core, 2 * target + core))
        received = lax.ppermute(sent, axis, pairs)
        to_start = jnp.exp(window_sum(ordered, place, 1, step - 1))[:, None, None]
        carried = carried + to_start * received
        if count + 1 < len(steps):
            to_end = jnp.exp(window_sum(ordered, place, 0, step - 1))[:, None, None]
            sent = sent + to_end * received
    return carried


def shards(queries, key_vectors, values, out_grad, log_decay):
    axis = "ctx"
    total, state, grad_state, pieces = prepare(queries, key_vectors, values, out_grad, log_decay)
    heads = total.shape[0]
    half = heads // 2
    chips = lax.axis_size(axis) // 2
    core = lax.axis_index(axis) % 2
    partner = [(2 * c + k, 2 * c + 1 - k) for c in range(chips) for k in range(2)]

    def other_half(a):
        return lax.dynamic_slice_in_dim(a, (1 - core) * half, half, 0)

    def own_half(a):
        return lax.dynamic_slice_in_dim(a, core * half, half, 0)

    sent = (total, other_half(state), other_half(grad_state))
    other_total, other_state, other_grad = lax.ppermute(sent, axis, partner)
    first = core == 0
    mine_state = own_half(state)
    mine_grad = own_half(grad_state)
    own_total_half = own_half(total)
    other_total_half = own_half(other_total)
    one = jnp.ones_like(own_total_half)
    fwd_a = jnp.where(first, jnp.exp(other_total_half), one)[:, None, None]
    fwd_b = jnp.where(first, one, jnp.exp(own_total_half))[:, None, None]
    chip_state = fwd_a * mine_state + fwd_b * other_state
    bwd_a = jnp.where(first, one, jnp.exp(other_total_half))[:, None, None]
    bwd_b = jnp.where(first, jnp.exp(own_total_half), one)[:, None, None]
    chip_grad = bwd_a * mine_grad + bwd_b * other_grad
    every_total = gather_rows(total, axis)
    chip_totals = every_total[0::2] + every_total[1::2]
    chip = lax.axis_index(axis) // 2
    steps = []
    step = 1
    while step < chips:
        steps.append(step)
        step *= 2
    turn = len(steps) // 2
    orders = (steps, steps[turn:] + steps[:turn])
    group = half // 2
    scans = []
    for chip_sum, reverse in ((chip_state, False), (chip_grad, True)):
        parts = []
        for g, order in enumerate(orders):
            group_totals = lax.dynamic_slice_in_dim(chip_totals, core * half + g * group, group, 1)
            parts.append(
                chip_scan(group_totals, chip_sum[g * group:(g + 1) * group], axis, chip, chips, reverse, order)
            )
        scans.append(jnp.concatenate(parts, 0))
    before, after = scans
    total_c0 = jnp.where(first, own_total_half, other_total_half)
    total_c1 = jnp.where(first, other_total_half, own_total_half)
    state_c0 = jnp.where(first, mine_state, other_state)
    grad_c1 = jnp.where(first, other_grad, mine_grad)
    fwd_core0 = before
    fwd_core1 = jnp.exp(total_c0)[:, None, None] * before + state_c0
    bwd_core0 = jnp.exp(total_c1)[:, None, None] * after + grad_c1
    bwd_core1 = after
    keep_fwd = jnp.where(first, fwd_core0, fwd_core1)
    keep_bwd = jnp.where(first, bwd_core0, bwd_core1)
    give_fwd = jnp.where(first, fwd_core1, fwd_core0)
    give_bwd = jnp.where(first, bwd_core1, bwd_core0)
    got_fwd, got_bwd = lax.ppermute((give_fwd, give_bwd), axis, partner)

    def assemble(keep, got):
        return jnp.where(first, jnp.concatenate([keep, got], 0), jnp.concatenate([got, keep], 0))

    return finish(pieces, assemble(keep_fwd, got_fwd), assemble(keep_bwd, got_bwd))


def solution(mesh):
    return jax.shard_map(
        shards,
        mesh=mesh,
        in_specs=(
            P(("dp", "ctx"), None),
            P(("dp", "ctx"), None),
            P(("dp", "ctx"), None),
            P(("dp", "ctx"), None),
            P(("dp", "ctx"), None),
        ),
        out_specs=(
            P(("dp", "ctx"), None),
            P(("dp", "ctx"), None),
            P(("dp", "ctx"), None),
            P(("dp", "ctx"), None),
        ),
        check_vma=False,
    )
```

```python
import jax
import jax.numpy as jnp
from jax import lax
from jax.sharding import PartitionSpec as P
from jax.experimental import pallas as pl
from jax.experimental.pallas import tpu as pltpu

SPAN = 64


def combine(earlier, latter):
    return (earlier[0] + latter[0], jnp.exp(latter[0])[..., None, None] * earlier[1] + latter[1])


def prepare(queries, key_vectors, values, out_grad, log_decay):
    highest = lax.Precision.HIGHEST
    length = queries.shape[0]
    heads = log_decay.shape[1]
    q_rows = queries.reshape(length, heads, -1).astype(jnp.float32)
    k_rows = key_vectors.reshape(length, heads, -1).astype(jnp.float32)
    v_rows = values.reshape(length, heads, -1).astype(jnp.float32)
    g_rows = out_grad.reshape(length, heads, -1).astype(jnp.float32)
    cumul = jnp.cumsum(log_decay.astype(jnp.float32), axis=0)
    total = cumul[-1]
    query_decay = jnp.exp(cumul)
    key_decay = jnp.exp(total[None, :] - cumul)
    state = jnp.einsum("she,shf->hef", k_rows * key_decay[..., None], v_rows, precision=highest)
    grad_state = jnp.einsum("the,thf->hef", q_rows * query_decay[..., None], g_rows, precision=highest)
    cumul_heads = jnp.transpose(cumul)
    pieces = (cumul_heads[:, None, :], cumul_heads[:, :, None], jnp.transpose(query_decay)[:, :, None],
              jnp.transpose(key_decay)[:, :, None])
    return total, state, grad_state, pieces


def head_kernel(q_ref, k_ref, v_ref, g_ref, row_ref, col_ref, qd_ref, kd_ref, s_ref, gs_ref,
                att_ref, qg_ref, kg_ref, vg_ref):
    highest = lax.Precision.HIGHEST
    f32 = jnp.float32
    q = q_ref[...].astype(f32)
    k = k_ref[...].astype(f32)
    v = v_ref[...].astype(f32)
    g = g_ref[...].astype(f32)
    size = q.shape[0]
    later = lax.broadcasted_iota(jnp.int32, (size, size), 0) >= lax.broadcasted_iota(jnp.int32, (size, size), 1)
    spread = col_ref[0] - row_ref[0]
    weights = jnp.where(later, jnp.exp(jnp.where(later, spread, 0.0)), 0.0)
    nt = (((1,), (1,)), ((), ()))
    scores = lax.dot_general(q, k, nt, precision=highest, preferred_element_type=f32) * weights
    grad_scores = lax.dot_general(g, v, nt, precision=highest, preferred_element_type=f32) * weights
    qd = qd_ref[0]
    kd = kd_ref[0]
    state = s_ref[0]
    grad_in = gs_ref[0]
    dot = lambda a, b: jnp.dot(a, b, precision=highest, preferred_element_type=f32)
    att_ref[...] = (dot(scores, v) + dot(q * qd, state)).astype(att_ref.dtype)
    qg_ref[...] = (dot(grad_scores, k) + lax.dot_general(g * qd, state, nt, precision=highest,
                                                         preferred_element_type=f32)).astype(qg_ref.dtype)
    kg_ref[...] = (dot(grad_scores.T, q) + lax.dot_general(v * kd, grad_in, nt, precision=highest,
                                                           preferred_element_type=f32)).astype(kg_ref.dtype)
    vg_ref[...] = (dot(scores.T, g) + dot(k * kd, grad_in)).astype(vg_ref.dtype)


def finish(inputs, pieces, state_in, grad_in):
    queries = inputs[0]
    length, width = queries.shape
    heads = state_in.shape[0]
    dk = width // heads
    rows, cols, qd, kd = pieces
    tile = pl.BlockSpec((length, dk), lambda h: (0, h))
    per_head = lambda a: pl.BlockSpec((1,) + a.shape[1:], lambda h: (h, 0, 0))
    out = jax.ShapeDtypeStruct((length, width), jnp.bfloat16)
    return pl.pallas_call(
        head_kernel,
        grid=(heads,),
        in_specs=[tile] * 4 + [per_head(a) for a in (rows, cols, qd, kd, state_in, grad_in)],
        out_specs=[tile] * 4,
        out_shape=[out] * 4,
        compiler_params=pltpu.CompilerParams(dimension_semantics=("arbitrary",)),
    )(*inputs, rows, cols, qd, kd, state_in, grad_in)


def gather_rows(row, axis):
    count = lax.axis_size(axis)
    me = lax.axis_index(axis)
    known = row[None]
    step = 1
    while step < count:
        pairs = [(i, (i + step) % count) for i in range(count)]
        known = jnp.concatenate([known, lax.ppermute(known, axis, pairs)], 0)
        step *= 2
    return known[(me - jnp.arange(count)) % count]


def window_sum(ordered, place, first, last):
    total = jnp.zeros_like(ordered[0])
    for back in range(first, last + 1):
        index = place - back
        picked = lax.dynamic_index_in_dim(ordered, jnp.maximum(index, 0), 0, False)
        total = total + jnp.where(index >= 0, picked, jnp.zeros_like(picked))
    return total


def chip_scan(chip_totals, state, axis, chip, chips, reverse, steps):
    direction = -1 if reverse else 1
    ordered = chip_totals[::-1] if reverse else chip_totals
    place = chips - 1 - chip if reverse else chip
    sent = state
    carried = jnp.zeros_like(state)
    for count, step in enumerate(steps):
        pairs = []
        for c in range(chips):
            target = c + direction * step
            if 0 <= target < chips:
                for core in range(2):
                    pairs.append((2 * c + core, 2 * target + core))
        received = lax.ppermute(sent, axis, pairs)
        to_start = jnp.exp(window_sum(ordered, place, 1, step - 1))[:, None, None]
        carried = carried + to_start * received
        if count + 1 < len(steps):
            to_end = jnp.exp(window_sum(ordered, place, 0, step - 1))[:, None, None]
            sent = sent + to_end * received
    return carried


def shards(queries, key_vectors, values, out_grad, log_decay):
    axis = "ctx"
    total, state, grad_state, pieces = prepare(queries, key_vectors, values, out_grad, log_decay)
    heads = total.shape[0]
    half = heads // 2
    chips = lax.axis_size(axis) // 2
    core = lax.axis_index(axis) % 2
    partner = [(2 * c + k, 2 * c + 1 - k) for c in range(chips) for k in range(2)]

    def other_half(a):
        return lax.dynamic_slice_in_dim(a, (1 - core) * half, half, 0)

    def own_half(a):
        return lax.dynamic_slice_in_dim(a, core * half, half, 0)

    sent = (total, other_half(state), other_half(grad_state))
    other_total, other_state, other_grad = lax.ppermute(sent, axis, partner)
    first = core == 0
    mine_state = own_half(state)
    mine_grad = own_half(grad_state)
    own_total_half = own_half(total)
    other_total_half = own_half(other_total)
    one = jnp.ones_like(own_total_half)
    fwd_a = jnp.where(first, jnp.exp(other_total_half), one)[:, None, None]
    fwd_b = jnp.where(first, one, jnp.exp(own_total_half))[:, None, None]
    chip_state = fwd_a * mine_state + fwd_b * other_state
    bwd_a = jnp.where(first, one, jnp.exp(other_total_half))[:, None, None]
    bwd_b = jnp.where(first, jnp.exp(own_total_half), one)[:, None, None]
    chip_grad = bwd_a * mine_grad + bwd_b * other_grad
    every_total = gather_rows(total, axis)
    chip_totals = every_total[0::2] + every_total[1::2]
    chip = lax.axis_index(axis) // 2
    steps = []
    step = 1
    while step < chips:
        steps.append(step)
        step *= 2
    turn = len(steps) // 2
    orders = (steps, steps[turn:] + steps[:turn])
    group = half // 2
    scans = []
    for chip_sum, reverse in ((chip_state, False), (chip_grad, True)):
        parts = []
        for g, order in enumerate(orders):
            group_totals = lax.dynamic_slice_in_dim(chip_totals, core * half + g * group, group, 1)
            parts.append(
                chip_scan(group_totals, chip_sum[g * group:(g + 1) * group], axis, chip, chips, reverse, order)
            )
        scans.append(jnp.concatenate(parts, 0))
    before, after = scans
    total_c0 = jnp.where(first, own_total_half, other_total_half)
    total_c1 = jnp.where(first, other_total_half, own_total_half)
    state_c0 = jnp.where(first, mine_state, other_state)
    grad_c1 = jnp.where(first, other_grad, mine_grad)
    fwd_core0 = before
    fwd_core1 = jnp.exp(total_c0)[:, None, None] * before + state_c0
    bwd_core0 = jnp.exp(total_c1)[:, None, None] * after + grad_c1
    bwd_core1 = after
    keep_fwd = jnp.where(first, fwd_core0, fwd_core1)
    keep_bwd = jnp.where(first, bwd_core0, bwd_core1)
    give_fwd = jnp.where(first, fwd_core1, fwd_core0)
    give_bwd = jnp.where(first, bwd_core1, bwd_core0)
    got_fwd, got_bwd = lax.ppermute((give_fwd, give_bwd), axis, partner)

    def assemble(keep, got):
        return jnp.where(first, jnp.concatenate([keep, got], 0), jnp.concatenate([got, keep], 0))

    inputs = (queries, key_vectors, values, out_grad)
    return tuple(finish(inputs, pieces, assemble(keep_fwd, got_fwd), assemble(keep_bwd, got_bwd)))


def solution(mesh):
    return jax.shard_map(
        shards,
        mesh=mesh,
        in_specs=(
            P(("dp", "ctx"), None),
            P(("dp", "ctx"), None),
            P(("dp", "ctx"), None),
            P(("dp", "ctx"), None),
            P(("dp", "ctx"), None),
        ),
        out_specs=(
            P(("dp", "ctx"), None),
            P(("dp", "ctx"), None),
            P(("dp", "ctx"), None),
            P(("dp", "ctx"), None),
        ),
        check_vma=False,
    )
```

```python
import jax
import jax.numpy as jnp
from jax import lax
from jax.sharding import PartitionSpec as P
from jax.experimental import pallas as pl
from jax.experimental.pallas import tpu as pltpu

SPAN = 64


def combine(earlier, latter):
    return (earlier[0] + latter[0], jnp.exp(latter[0])[..., None, None] * earlier[1] + latter[1])


def prepare(queries, key_vectors, values, out_grad, log_decay):
    highest = lax.Precision.HIGHEST
    length = queries.shape[0]
    heads = log_decay.shape[1]
    q_rows = queries.reshape(length, heads, -1).astype(jnp.float32)
    k_rows = key_vectors.reshape(length, heads, -1).astype(jnp.float32)
    v_rows = values.reshape(length, heads, -1).astype(jnp.float32)
    g_rows = out_grad.reshape(length, heads, -1).astype(jnp.float32)
    cumul = jnp.cumsum(log_decay.astype(jnp.float32), axis=0)
    total = cumul[-1]
    query_decay = jnp.exp(cumul)
    key_decay = jnp.exp(total[None, :] - cumul)
    state = jnp.einsum("she,shf->hef", k_rows * key_decay[..., None], v_rows, precision=highest)
    grad_state = jnp.einsum("the,thf->hef", q_rows * query_decay[..., None], g_rows, precision=highest)
    pieces = jnp.transpose(cumul)
    total = jnp.sum(log_decay.astype(jnp.float32), axis=0)
    return total, state, grad_state, pieces


def split(x):
    high = x.astype(jnp.bfloat16)
    return high, (x - high.astype(jnp.float32)).astype(jnp.bfloat16)


def head_kernel(q_ref, k_ref, v_ref, g_ref, cum_ref, s_ref, gs_ref, att_ref, qg_ref, kg_ref, vg_ref):
    f32 = jnp.float32
    nn = (((1,), (0,)), ((), ()))
    nt = (((1,), (1,)), ((), ()))

    def mm(a, b, dims):
        return lax.dot_general(a, b, dims, preferred_element_type=f32)

    def mm_right(a, b, dims):
        high, low = split(b)
        return mm(a, high, dims) + mm(a, low, dims)

    def mm_left(a, b, dims):
        high, low = split(a)
        return mm(high, b, dims) + mm(low, b, dims)

    size = q_ref.shape[0]
    block = cum_ref.shape[0]
    dk = q_ref.shape[1] // block
    later = lax.broadcasted_iota(jnp.int32, (size, size), 0) >= lax.broadcasted_iota(jnp.int32, (size, size), 1)
    for j in range(block):
        cols = slice(j * dk, (j + 1) * dk)
        q = q_ref[:, cols]
        k = k_ref[:, cols]
        v = v_ref[:, cols]
        g = g_ref[:, cols]
        row = cum_ref[j:j + 1, :]
        grid_row = jnp.broadcast_to(row, (size, size))
        col = jnp.sum(jnp.where(later & (~(lax.broadcasted_iota(jnp.int32, (size, size), 0) >
                                           lax.broadcasted_iota(jnp.int32, (size, size), 1))), grid_row, 0.0),
                      axis=1, keepdims=True)
        last = row[:, size - 1:size]
        weights = jnp.where(later, jnp.exp(jnp.where(later, col - row, 0.0)), 0.0)
        scores = mm(q, k, nt) * weights
        grad_scores = mm(g, v, nt) * weights
        qd = jnp.exp(col)
        kd = jnp.exp(last - col)
        state = s_ref[j]
        grad_in = gs_ref[j]
        att_ref[:, cols] = (mm_left(scores, v, nn) + qd * mm_right(q, state, nn)).astype(att_ref.dtype)
        qg_ref[:, cols] = (mm_left(grad_scores, k, nn) + qd * mm_right(g, state, nt)).astype(qg_ref.dtype)
        kg_ref[:, cols] = (mm_left(grad_scores.T, q, nn) + kd * mm_right(v, grad_in, nt)).astype(kg_ref.dtype)
        vg_ref[:, cols] = (mm_left(scores.T, g, nn) + kd * mm_right(k, grad_in, nn)).astype(vg_ref.dtype)


def finish(inputs, cumul_heads, state_in, grad_in):
    queries = inputs[0]
    length, width = queries.shape
    heads = state_in.shape[0]
    dk = width // heads
    block = 8
    tile = pl.BlockSpec((length, block * dk), lambda h: (0, h))
    states = pl.BlockSpec((block, dk, dk), lambda h: (h, 0, 0))
    out = jax.ShapeDtypeStruct((length, width), jnp.bfloat16)
    return pl.pallas_call(
        head_kernel,
        grid=(heads // block,),
        in_specs=[tile] * 4 + [pl.BlockSpec((block, length), lambda h: (h, 0)), states, states],
        out_specs=[tile] * 4,
        out_shape=[out] * 4,
        compiler_params=pltpu.CompilerParams(dimension_semantics=("arbitrary",)),
    )(*inputs, cumul_heads, state_in, grad_in)


def gather_rows(row, axis):
    count = lax.axis_size(axis)
    me = lax.axis_index(axis)
    known = row[None]
    step = 1
    while step < count:
        pairs = [(i, (i + step) % count) for i in range(count)]
        known = jnp.concatenate([known, lax.ppermute(known, axis, pairs)], 0)
        step *= 2
    return known[(me - jnp.arange(count)) % count]


def window_sum(ordered, place, first, last):
    total = jnp.zeros_like(ordered[0])
    for back in range(first, last + 1):
        index = place - back
        picked = lax.dynamic_index_in_dim(ordered, jnp.maximum(index, 0), 0, False)
        total = total + jnp.where(index >= 0, picked, jnp.zeros_like(picked))
    return total


def chip_scan(chip_totals, state, axis, chip, chips, reverse, steps):
    direction = -1 if reverse else 1
    ordered = chip_totals[::-1] if reverse else chip_totals
    place = chips - 1 - chip if reverse else chip
    sent = state
    carried = jnp.zeros_like(state)
    for count, step in enumerate(steps):
        pairs = []
        for c in range(chips):
            target = c + direction * step
            if 0 <= target < chips:
                for core in range(2):
                    pairs.append((2 * c + core, 2 * target + core))
        received = lax.ppermute(sent, axis, pairs)
        to_start = jnp.exp(window_sum(ordered, place, 1, step - 1))[:, None, None]
        carried = carried + to_start * received
        if count + 1 < len(steps):
            to_end = jnp.exp(window_sum(ordered, place, 0, step - 1))[:, None, None]
            sent = sent + to_end * received
    return carried


def shards(queries, key_vectors, values, out_grad, log_decay):
    axis = "ctx"
    total, state, grad_state, pieces = prepare(queries, key_vectors, values, out_grad, log_decay)
    heads = total.shape[0]
    half = heads // 2
    chips = lax.axis_size(axis) // 2
    core = lax.axis_index(axis) % 2
    partner = [(2 * c + k, 2 * c + 1 - k) for c in range(chips) for k in range(2)]

    def other_half(a):
        return lax.dynamic_slice_in_dim(a, (1 - core) * half, half, 0)

    def own_half(a):
        return lax.dynamic_slice_in_dim(a, core * half, half, 0)

    sent = (total, other_half(state), other_half(grad_state))
    other_total, other_state, other_grad = lax.ppermute(sent, axis, partner)
    first = core == 0
    mine_state = own_half(state)
    mine_grad = own_half(grad_state)
    own_total_half = own_half(total)
    other_total_half = own_half(other_total)
    one = jnp.ones_like(own_total_half)
    fwd_a = jnp.where(first, jnp.exp(other_total_half), one)[:, None, None]
    fwd_b = jnp.where(first, one, jnp.exp(own_total_half))[:, None, None]
    chip_state = fwd_a * mine_state + fwd_b * other_state
    bwd_a = jnp.where(first, one, jnp.exp(other_total_half))[:, None, None]
    bwd_b = jnp.where(first, jnp.exp(own_total_half), one)[:, None, None]
    chip_grad = bwd_a * mine_grad + bwd_b * other_grad
    every_total = gather_rows(total, axis)
    chip_totals = every_total[0::2] + every_total[1::2]
    chip = lax.axis_index(axis) // 2
    steps = []
    step = 1
    while step < chips:
        steps.append(step)
        step *= 2
    turn = len(steps) // 2
    orders = (steps, steps[turn:] + steps[:turn])
    group = half // 2
    scans = []
    for chip_sum, reverse in ((chip_state, False), (chip_grad, True)):
        parts = []
        for g, order in enumerate(orders):
            group_totals = lax.dynamic_slice_in_dim(chip_totals, core * half + g * group, group, 1)
            parts.append(
                chip_scan(group_totals, chip_sum[g * group:(g + 1) * group], axis, chip, chips, reverse, order)
            )
        scans.append(jnp.concatenate(parts, 0))
    before, after = scans
    total_c0 = jnp.where(first, own_total_half, other_total_half)
    total_c1 = jnp.where(first, other_total_half, own_total_half)
    state_c0 = jnp.where(first, mine_state, other_state)
    grad_c1 = jnp.where(first, other_grad, mine_grad)
    fwd_core0 = before
    fwd_core1 = jnp.exp(total_c0)[:, None, None] * before + state_c0
    bwd_core0 = jnp.exp(total_c1)[:, None, None] * after + grad_c1
    bwd_core1 = after
    keep_fwd = jnp.where(first, fwd_core0, fwd_core1)
    keep_bwd = jnp.where(first, bwd_core0, bwd_core1)
    give_fwd = jnp.where(first, fwd_core1, fwd_core0)
    give_bwd = jnp.where(first, bwd_core1, bwd_core0)
    got_fwd, got_bwd = lax.ppermute((give_fwd, give_bwd), axis, partner)

    def assemble(keep, got):
        return jnp.where(first, jnp.concatenate([keep, got], 0), jnp.concatenate([got, keep], 0))

    inputs = (queries, key_vectors, values, out_grad)
    return tuple(finish(inputs, pieces, assemble(keep_fwd, got_fwd), assemble(keep_bwd, got_bwd)))


def solution(mesh):
    return jax.shard_map(
        shards,
        mesh=mesh,
        in_specs=(
            P(("dp", "ctx"), None),
            P(("dp", "ctx"), None),
            P(("dp", "ctx"), None),
            P(("dp", "ctx"), None),
            P(("dp", "ctx"), None),
        ),
        out_specs=(
            P(("dp", "ctx"), None),
            P(("dp", "ctx"), None),
            P(("dp", "ctx"), None),
            P(("dp", "ctx"), None),
        ),
        check_vma=False,
    )
```

```python
import jax
import jax.numpy as jnp
from jax import lax
from jax.sharding import PartitionSpec as P
from jax.experimental import pallas as pl
from jax.experimental.pallas import tpu as pltpu

SPAN = 64


def combine(earlier, latter):
    return (earlier[0] + latter[0], jnp.exp(latter[0])[..., None, None] * earlier[1] + latter[1])


def prepare(queries, key_vectors, values, out_grad, log_decay):
    highest = lax.Precision.HIGHEST
    length = queries.shape[0]
    heads = log_decay.shape[1]
    q_rows = queries.reshape(length, heads, -1).astype(jnp.float32)
    k_rows = key_vectors.reshape(length, heads, -1).astype(jnp.float32)
    v_rows = values.reshape(length, heads, -1).astype(jnp.float32)
    g_rows = out_grad.reshape(length, heads, -1).astype(jnp.float32)
    cumul = jnp.cumsum(log_decay.astype(jnp.float32), axis=0)
    total = cumul[-1]
    query_decay = jnp.exp(cumul)
    key_decay = jnp.exp(total[None, :] - cumul)
    state = jnp.einsum("she,shf->hef", k_rows * key_decay[..., None], v_rows, precision=highest)
    grad_state = jnp.einsum("the,thf->hef", q_rows * query_decay[..., None], g_rows, precision=highest)
    pieces = jnp.transpose(cumul)
    total = jnp.sum(log_decay.astype(jnp.float32), axis=0)
    return total, state, grad_state, pieces


def split(x):
    high = x.astype(jnp.bfloat16)
    return high, (x - high.astype(jnp.float32)).astype(jnp.bfloat16)


def head_kernel(q_ref, k_ref, v_ref, g_ref, cum_ref, s_ref, gs_ref, att_ref, qg_ref, kg_ref, vg_ref):
    f32 = jnp.float32
    nn = (((1,), (0,)), ((), ()))
    nt = (((1,), (1,)), ((), ()))

    def mm(a, b, dims):
        return lax.dot_general(a, b, dims, preferred_element_type=f32)

    def mm_right(a, b, dims):
        high, low = split(b)
        return mm(a, high, dims) + mm(a, low, dims)

    def mm_left(a, b, dims):
        high, low = split(a)
        return mm(high, b, dims) + mm(low, b, dims)

    size = q_ref.shape[0]
    block = cum_ref.shape[0]
    dk = q_ref.shape[1] // block
    later = lax.broadcasted_iota(jnp.int32, (size, size), 0) >= lax.broadcasted_iota(jnp.int32, (size, size), 1)
    for j in range(block):
        cols = slice(j * dk, (j + 1) * dk)
        q = q_ref[:, cols]
        k = k_ref[:, cols]
        v = v_ref[:, cols]
        g = g_ref[:, cols]
        row = cum_ref[j:j + 1, :]
        grid_row = jnp.broadcast_to(row, (size, size))
        col = jnp.sum(jnp.where(later & (~(lax.broadcasted_iota(jnp.int32, (size, size), 0) >
                                           lax.broadcasted_iota(jnp.int32, (size, size), 1))), grid_row, 0.0),
                      axis=1, keepdims=True)
        last = row[:, size - 1:size]
        weights = jnp.where(later, jnp.exp(jnp.where(later, col - row, 0.0)), 0.0)
        scores = mm(q, k, nt) * weights
        grad_scores = mm(g, v, nt) * weights
        qd = jnp.exp(col)
        kd = jnp.exp(last - col)
        state = s_ref[j]
        grad_in = gs_ref[j]
        att_ref[:, cols] = (mm_left(scores, v, nn) + qd * mm_right(q, state, nn)).astype(att_ref.dtype)
        qg_ref[:, cols] = (mm_left(grad_scores, k, nn) + qd * mm_right(g, state, nt)).astype(qg_ref.dtype)
        kg_ref[:, cols] = (mm_left(grad_scores.T, q, nn) + kd * mm_right(v, grad_in, nt)).astype(kg_ref.dtype)
        vg_ref[:, cols] = (mm_left(scores.T, g, nn) + kd * mm_right(k, grad_in, nn)).astype(vg_ref.dtype)


def finish(inputs, cumul_heads, state_in, grad_in):
    queries = inputs[0]
    length, width = queries.shape
    heads = state_in.shape[0]
    dk = width // heads
    block = 8
    tile = pl.BlockSpec((length, block * dk), lambda h: (0, h))
    states = pl.BlockSpec((block, dk, dk), lambda h: (h, 0, 0))
    out = jax.ShapeDtypeStruct((length, width), jnp.bfloat16)
    return pl.pallas_call(
        head_kernel,
        grid=(heads // block,),
        in_specs=[tile] * 4 + [pl.BlockSpec((block, length), lambda h: (h, 0)), states, states],
        out_specs=[tile] * 4,
        out_shape=[out] * 4,
        compiler_params=pltpu.CompilerParams(dimension_semantics=("arbitrary",)),
    )(*inputs, cumul_heads, state_in, grad_in)


def gather_rows(row, axis):
    count = lax.axis_size(axis)
    me = lax.axis_index(axis)
    known = row[None]
    step = 1
    while step < count:
        pairs = [(i, (i + step) % count) for i in range(count)]
        known = jnp.concatenate([known, lax.ppermute(known, axis, pairs)], 0)
        step *= 2
    return known[(me - jnp.arange(count)) % count]


def window_sum(ordered, place, first, last):
    total = jnp.zeros_like(ordered[0])
    for back in range(first, last + 1):
        index = place - back
        picked = lax.dynamic_index_in_dim(ordered, jnp.maximum(index, 0), 0, False)
        total = total + jnp.where(index >= 0, picked, jnp.zeros_like(picked))
    return total


def chip_scan(chip_totals, state, axis, chip, chips, reverse, steps):
    direction = -1 if reverse else 1
    ordered = chip_totals[::-1] if reverse else chip_totals
    place = chips - 1 - chip if reverse else chip
    sent = state
    carried = jnp.zeros_like(state)
    for count, step in enumerate(steps):
        pairs = []
        for c in range(chips):
            target = c + direction * step
            if 0 <= target < chips:
                for core in range(2):
                    pairs.append((2 * c + core, 2 * target + core))
        received = lax.ppermute(sent, axis, pairs)
        to_start = jnp.exp(window_sum(ordered, place, 1, step - 1))[:, None, None]
        carried = carried + to_start * received
        if count + 1 < len(steps):
            to_end = jnp.exp(window_sum(ordered, place, 0, step - 1))[:, None, None]
            sent = sent + to_end * received
    return carried


def shards(queries, key_vectors, values, out_grad, log_decay):
    axis = "ctx"
    total, state, grad_state, pieces = prepare(queries, key_vectors, values, out_grad, log_decay)
    heads = total.shape[0]
    half = heads // 2
    chips = lax.axis_size(axis) // 2
    core = lax.axis_index(axis) % 2
    partner = [(2 * c + k, 2 * c + 1 - k) for c in range(chips) for k in range(2)]

    def other_half(a):
        return lax.dynamic_slice_in_dim(a, (1 - core) * half, half, 0)

    def own_half(a):
        return lax.dynamic_slice_in_dim(a, core * half, half, 0)

    sent = (total, other_half(state), other_half(grad_state))
    other_total, other_state, other_grad = lax.ppermute(sent, axis, partner)
    first = core == 0
    mine_state = own_half(state)
    mine_grad = own_half(grad_state)
    own_total_half = own_half(total)
    other_total_half = own_half(other_total)
    one = jnp.ones_like(own_total_half)
    fwd_a = jnp.where(first, jnp.exp(other_total_half), one)[:, None, None]
    fwd_b = jnp.where(first, one, jnp.exp(own_total_half))[:, None, None]
    chip_state = fwd_a * mine_state + fwd_b * other_state
    bwd_a = jnp.where(first, one, jnp.exp(other_total_half))[:, None, None]
    bwd_b = jnp.where(first, jnp.exp(own_total_half), one)[:, None, None]
    chip_grad = bwd_a * mine_grad + bwd_b * other_grad
    padded = jnp.zeros((64, 128), total.dtype).at[0, :total.shape[0]].set(total)
    every_total = lax.all_gather(padded, axis)[:, 0, :total.shape[0]]
    chip_totals = every_total[0::2] + every_total[1::2]
    chip = lax.axis_index(axis) // 2
    steps = []
    step = 1
    while step < chips:
        steps.append(step)
        step *= 2
    turn = len(steps) // 2
    orders = (steps, steps[turn:] + steps[:turn])
    group = half // 2
    scans = []
    for chip_sum, reverse in ((chip_state, False), (chip_grad, True)):
        parts = []
        for g, order in enumerate(orders):
            group_totals = lax.dynamic_slice_in_dim(chip_totals, core * half + g * group, group, 1)
            parts.append(
                chip_scan(group_totals, chip_sum[g * group:(g + 1) * group], axis, chip, chips, reverse, order)
            )
        scans.append(jnp.concatenate(parts, 0))
    before, after = scans
    total_c0 = jnp.where(first, own_total_half, other_total_half)
    total_c1 = jnp.where(first, other_total_half, own_total_half)
    state_c0 = jnp.where(first, mine_state, other_state)
    grad_c1 = jnp.where(first, other_grad, mine_grad)
    fwd_core0 = before
    fwd_core1 = jnp.exp(total_c0)[:, None, None] * before + state_c0
    bwd_core0 = jnp.exp(total_c1)[:, None, None] * after + grad_c1
    bwd_core1 = after
    keep_fwd = jnp.where(first, fwd_core0, fwd_core1)
    keep_bwd = jnp.where(first, bwd_core0, bwd_core1)
    give_fwd = jnp.where(first, fwd_core1, fwd_core0)
    give_bwd = jnp.where(first, bwd_core1, bwd_core0)
    got_fwd, got_bwd = lax.ppermute((give_fwd, give_bwd), axis, partner)

    def assemble(keep, got):
        return jnp.where(first, jnp.concatenate([keep, got], 0), jnp.concatenate([got, keep], 0))

    inputs = (queries, key_vectors, values, out_grad)
    return tuple(finish(inputs, pieces, assemble(keep_fwd, got_fwd), assemble(keep_bwd, got_bwd)))


def solution(mesh):
    return jax.shard_map(
        shards,
        mesh=mesh,
        in_specs=(
            P(("dp", "ctx"), None),
            P(("dp", "ctx"), None),
            P(("dp", "ctx"), None),
            P(("dp", "ctx"), None),
            P(("dp", "ctx"), None),
        ),
        out_specs=(
            P(("dp", "ctx"), None),
            P(("dp", "ctx"), None),
            P(("dp", "ctx"), None),
            P(("dp", "ctx"), None),
        ),
        check_vma=False,
    )
```

```python
import jax
import jax.numpy as jnp
from jax import lax
from jax.sharding import PartitionSpec as P
from jax.experimental import pallas as pl
from jax.experimental.pallas import tpu as pltpu

SPAN = 64


def combine(earlier, latter):
    return (earlier[0] + latter[0], jnp.exp(latter[0])[..., None, None] * earlier[1] + latter[1])


def prepare(queries, key_vectors, values, out_grad, log_decay):
    highest = lax.Precision.HIGHEST
    length = queries.shape[0]
    heads = log_decay.shape[1]
    q_rows = queries.reshape(length, heads, -1).astype(jnp.float32)
    k_rows = key_vectors.reshape(length, heads, -1).astype(jnp.float32)
    v_rows = values.reshape(length, heads, -1).astype(jnp.float32)
    g_rows = out_grad.reshape(length, heads, -1).astype(jnp.float32)
    cumul = jnp.cumsum(log_decay.astype(jnp.float32), axis=0)
    total = cumul[-1]
    query_decay = jnp.exp(cumul)
    key_decay = jnp.exp(total[None, :] - cumul)
    state = jnp.einsum("she,shf->hef", k_rows * key_decay[..., None], v_rows, precision=highest)
    grad_state = jnp.einsum("the,thf->hef", q_rows * query_decay[..., None], g_rows, precision=highest)
    pieces = jnp.transpose(cumul)
    total = jnp.sum(log_decay.astype(jnp.float32), axis=0)
    return total, state, grad_state, pieces


def split(x):
    high = x.astype(jnp.bfloat16)
    return high, (x - high.astype(jnp.float32)).astype(jnp.bfloat16)


def head_kernel(q_ref, k_ref, v_ref, g_ref, cum_ref, s_ref, gs_ref, att_ref, qg_ref, kg_ref, vg_ref):
    f32 = jnp.float32
    nn = (((1,), (0,)), ((), ()))
    nt = (((1,), (1,)), ((), ()))

    def mm(a, b, dims):
        return lax.dot_general(a, b, dims, preferred_element_type=f32)

    def mm_right(a, b, dims):
        high, low = split(b)
        return mm(a, high, dims) + mm(a, low, dims)

    def mm_left(a, b, dims):
        high, low = split(a)
        return mm(high, b, dims) + mm(low, b, dims)

    size = q_ref.shape[0]
    block = cum_ref.shape[0]
    dk = q_ref.shape[1] // block
    later = lax.broadcasted_iota(jnp.int32, (size, size), 0) >= lax.broadcasted_iota(jnp.int32, (size, size), 1)
    for j in range(block):
        cols = slice(j * dk, (j + 1) * dk)
        q = q_ref[:, cols]
        k = k_ref[:, cols]
        v = v_ref[:, cols]
        g = g_ref[:, cols]
        row = cum_ref[j:j + 1, :]
        grid_row = jnp.broadcast_to(row, (size, size))
        col = jnp.sum(jnp.where(later & (~(lax.broadcasted_iota(jnp.int32, (size, size), 0) >
                                           lax.broadcasted_iota(jnp.int32, (size, size), 1))), grid_row, 0.0),
                      axis=1, keepdims=True)
        last = row[:, size - 1:size]
        weights = jnp.where(later, jnp.exp(jnp.where(later, col - row, 0.0)), 0.0)
        scores = mm(q, k, nt) * weights
        grad_scores = mm(g, v, nt) * weights
        qd = jnp.exp(col)
        kd = jnp.exp(last - col)
        state = s_ref[j]
        grad_in = gs_ref[j]
        att_ref[:, cols] = (mm_left(scores, v, nn) + qd * mm_right(q, state, nn)).astype(att_ref.dtype)
        qg_ref[:, cols] = (mm_left(grad_scores, k, nn) + qd * mm_right(g, state, nt)).astype(qg_ref.dtype)
        kg_ref[:, cols] = (mm_left(grad_scores.T, q, nn) + kd * mm_right(v, grad_in, nt)).astype(kg_ref.dtype)
        vg_ref[:, cols] = (mm_left(scores.T, g, nn) + kd * mm_right(k, grad_in, nn)).astype(vg_ref.dtype)


def finish(inputs, cumul_heads, state_in, grad_in):
    queries = inputs[0]
    length, width = queries.shape
    heads = state_in.shape[0]
    dk = width // heads
    block = 8
    tile = pl.BlockSpec((length, block * dk), lambda h: (0, h))
    states = pl.BlockSpec((block, dk, dk), lambda h: (h, 0, 0))
    out = jax.ShapeDtypeStruct((length, width), jnp.bfloat16)
    return pl.pallas_call(
        head_kernel,
        grid=(heads // block,),
        in_specs=[tile] * 4 + [pl.BlockSpec((block, length), lambda h: (h, 0)), states, states],
        out_specs=[tile] * 4,
        out_shape=[out] * 4,
        compiler_params=pltpu.CompilerParams(dimension_semantics=("arbitrary",)),
    )(*inputs, cumul_heads, state_in, grad_in)


def gather_rows(row, axis):
    count = lax.axis_size(axis)
    me = lax.axis_index(axis)
    known = row[None]
    early = None
    step = 1
    while step < count:
        pairs = [(i, (i + step) % count) for i in range(count)]
        known = jnp.concatenate([known, lax.ppermute(known, axis, pairs)], 0)
        early = known if early is None else early
        step *= 2
    return known[(me - jnp.arange(count)) % count], early


def window_sum(ordered, place, first, last):
    total = jnp.zeros_like(ordered[0])
    for back in range(first, last + 1):
        index = place - back
        picked = lax.dynamic_index_in_dim(ordered, jnp.maximum(index, 0), 0, False)
        total = total + jnp.where(index >= 0, picked, jnp.zeros_like(picked))
    return total


def chip_scan(chip_totals, state, axis, chip, chips, reverse, steps):
    direction = -1 if reverse else 1
    ordered = chip_totals[::-1] if reverse else chip_totals
    place = chips - 1 - chip if reverse else chip
    sent = state
    carried = jnp.zeros_like(state)
    for count, step in enumerate(steps):
        pairs = []
        for c in range(chips):
            target = c + direction * step
            if 0 <= target < chips:
                for core in range(2):
                    pairs.append((2 * c + core, 2 * target + core))
        received = lax.ppermute(sent, axis, pairs)
        to_start = jnp.exp(window_sum(ordered, place, 1, step - 1))[:, None, None]
        carried = carried + to_start * received
        if count + 1 < len(steps):
            to_end = jnp.exp(window_sum(ordered, place, 0, step - 1))[:, None, None]
            sent = sent + to_end * received
    return carried


def shards(queries, key_vectors, values, out_grad, log_decay):
    axis = "ctx"
    total = jnp.sum(log_decay.astype(jnp.float32), axis=0)
    every_total, early = gather_rows(total, axis)
    _, queries, key_vectors, values, out_grad = lax.optimization_barrier(
        (early, queries, key_vectors, values, out_grad))
    _, state, grad_state, pieces = prepare(queries, key_vectors, values, out_grad, log_decay)
    heads = total.shape[0]
    half = heads // 2
    chips = lax.axis_size(axis) // 2
    core = lax.axis_index(axis) % 2
    partner = [(2 * c + k, 2 * c + 1 - k) for c in range(chips) for k in range(2)]

    def other_half(a):
        return lax.dynamic_slice_in_dim(a, (1 - core) * half, half, 0)

    def own_half(a):
        return lax.dynamic_slice_in_dim(a, core * half, half, 0)

    sent = (total, other_half(state), other_half(grad_state))
    other_total, other_state, other_grad = lax.ppermute(sent, axis, partner)
    first = core == 0
    mine_state = own_half(state)
    mine_grad = own_half(grad_state)
    own_total_half = own_half(total)
    other_total_half = own_half(other_total)
    one = jnp.ones_like(own_total_half)
    fwd_a = jnp.where(first, jnp.exp(other_total_half), one)[:, None, None]
    fwd_b = jnp.where(first, one, jnp.exp(own_total_half))[:, None, None]
    chip_state = fwd_a * mine_state + fwd_b * other_state
    bwd_a = jnp.where(first, one, jnp.exp(other_total_half))[:, None, None]
    bwd_b = jnp.where(first, jnp.exp(own_total_half), one)[:, None, None]
    chip_grad = bwd_a * mine_grad + bwd_b * other_grad
    chip_totals = every_total[0::2] + every_total[1::2]
    chip = lax.axis_index(axis) // 2
    steps = []
    step = 1
    while step < chips:
        steps.append(step)
        step *= 2
    turn = len(steps) // 2
    orders = (steps, steps[turn:] + steps[:turn])
    group = half // 2
    scans = []
    for chip_sum, reverse in ((chip_state, False), (chip_grad, True)):
        parts = []
        for g, order in enumerate(orders):
            group_totals = lax.dynamic_slice_in_dim(chip_totals, core * half + g * group, group, 1)
            parts.append(
                chip_scan(group_totals, chip_sum[g * group:(g + 1) * group], axis, chip, chips, reverse, order)
            )
        scans.append(jnp.concatenate(parts, 0))
    before, after = scans
    total_c0 = jnp.where(first, own_total_half, other_total_half)
    total_c1 = jnp.where(first, other_total_half, own_total_half)
    state_c0 = jnp.where(first, mine_state, other_state)
    grad_c1 = jnp.where(first, other_grad, mine_grad)
    fwd_core0 = before
    fwd_core1 = jnp.exp(total_c0)[:, None, None] * before + state_c0
    bwd_core0 = jnp.exp(total_c1)[:, None, None] * after + grad_c1
    bwd_core1 = after
    keep_fwd = jnp.where(first, fwd_core0, fwd_core1)
    keep_bwd = jnp.where(first, bwd_core0, bwd_core1)
    give_fwd = jnp.where(first, fwd_core1, fwd_core0)
    give_bwd = jnp.where(first, bwd_core1, bwd_core0)
    got_fwd, got_bwd = lax.ppermute((give_fwd, give_bwd), axis, partner)

    def assemble(keep, got):
        return jnp.where(first, jnp.concatenate([keep, got], 0), jnp.concatenate([got, keep], 0))

    inputs = (queries, key_vectors, values, out_grad)
    return tuple(finish(inputs, pieces, assemble(keep_fwd, got_fwd), assemble(keep_bwd, got_bwd)))


def solution(mesh):
    return jax.shard_map(
        shards,
        mesh=mesh,
        in_specs=(
            P(("dp", "ctx"), None),
            P(("dp", "ctx"), None),
            P(("dp", "ctx"), None),
            P(("dp", "ctx"), None),
            P(("dp", "ctx"), None),
        ),
        out_specs=(
            P(("dp", "ctx"), None),
            P(("dp", "ctx"), None),
            P(("dp", "ctx"), None),
            P(("dp", "ctx"), None),
        ),
        check_vma=False,
    )
```

```python
import jax
import jax.numpy as jnp
from jax import lax
from jax.sharding import PartitionSpec as P
from jax.experimental import pallas as pl
from jax.experimental.pallas import tpu as pltpu

SPAN = 64


def combine(earlier, latter):
    return (earlier[0] + latter[0], jnp.exp(latter[0])[..., None, None] * earlier[1] + latter[1])


def prepare(queries, key_vectors, values, out_grad, log_decay):
    highest = lax.Precision.HIGHEST
    length = queries.shape[0]
    heads = log_decay.shape[1]
    q_rows = queries.reshape(length, heads, -1).astype(jnp.float32)
    k_rows = key_vectors.reshape(length, heads, -1).astype(jnp.float32)
    v_rows = values.reshape(length, heads, -1).astype(jnp.float32)
    g_rows = out_grad.reshape(length, heads, -1).astype(jnp.float32)
    cumul = jnp.cumsum(log_decay.astype(jnp.float32), axis=0)
    total = cumul[-1]
    query_decay = jnp.exp(cumul)
    key_decay = jnp.exp(total[None, :] - cumul)
    state = jnp.einsum("she,shf->hef", k_rows * key_decay[..., None], v_rows, precision=highest)
    grad_state = jnp.einsum("the,thf->hef", q_rows * query_decay[..., None], g_rows, precision=highest)
    pieces = jnp.transpose(cumul)
    total = jnp.sum(log_decay.astype(jnp.float32), axis=0)
    return total, state, grad_state, pieces


def split(x):
    high = x.astype(jnp.bfloat16)
    return high, (x - high.astype(jnp.float32)).astype(jnp.bfloat16)


def head_kernel(core_ref, q_ref, k_ref, v_ref, g_ref, cum_ref, keep_ref, got_ref, keep_g_ref, got_g_ref,
                att_ref, qg_ref, kg_ref, vg_ref):
    f32 = jnp.float32
    nn = (((1,), (0,)), ((), ()))
    nt = (((1,), (1,)), ((), ()))

    def mm(a, b, dims):
        return lax.dot_general(a, b, dims, preferred_element_type=f32)

    def mm_right(a, b, dims):
        high, low = split(b)
        return mm(a, high, dims) + mm(a, low, dims)

    def mm_left(a, b, dims):
        high, low = split(a)
        return mm(high, b, dims) + mm(low, b, dims)

    size = q_ref.shape[0]
    block = cum_ref.shape[0]
    dk = q_ref.shape[1] // block
    later = lax.broadcasted_iota(jnp.int32, (size, size), 0) >= lax.broadcasted_iota(jnp.int32, (size, size), 1)
    kept = pl.program_id(0) // (keep_ref.shape[0] * 2 // block) == core_ref[0]
    for j in range(block):
        cols = slice(j * dk, (j + 1) * dk)
        q = q_ref[:, cols]
        k = k_ref[:, cols]
        v = v_ref[:, cols]
        g = g_ref[:, cols]
        row = cum_ref[j:j + 1, :]
        grid_row = jnp.broadcast_to(row, (size, size))
        col = jnp.sum(jnp.where(later & (~(lax.broadcasted_iota(jnp.int32, (size, size), 0) >
                                           lax.broadcasted_iota(jnp.int32, (size, size), 1))), grid_row, 0.0),
                      axis=1, keepdims=True)
        last = row[:, size - 1:size]
        weights = jnp.where(later, jnp.exp(jnp.where(later, col - row, 0.0)), 0.0)
        scores = mm(q, k, nt) * weights
        grad_scores = mm(g, v, nt) * weights
        qd = jnp.exp(col)
        kd = jnp.exp(last - col)
        state = jnp.where(kept, keep_ref[j], got_ref[j])
        grad_in = jnp.where(kept, keep_g_ref[j], got_g_ref[j])
        att_ref[:, cols] = (mm_left(scores, v, nn) + qd * mm_right(q, state, nn)).astype(att_ref.dtype)
        qg_ref[:, cols] = (mm_left(grad_scores, k, nn) + qd * mm_right(g, state, nt)).astype(qg_ref.dtype)
        kg_ref[:, cols] = (mm_left(grad_scores.T, q, nn) + kd * mm_right(v, grad_in, nt)).astype(kg_ref.dtype)
        vg_ref[:, cols] = (mm_left(scores.T, g, nn) + kd * mm_right(k, grad_in, nn)).astype(vg_ref.dtype)


def finish(inputs, cumul_heads, core, halves):
    queries = inputs[0]
    length, width = queries.shape
    half = halves[0].shape[0]
    heads = 2 * half
    dk = width // heads
    block = 8
    steps = half // block
    tile = pl.BlockSpec((length, block * dk), lambda h, c: (0, h))
    states = pl.BlockSpec((block, dk, dk), lambda h, c: (h % steps, 0, 0))
    out = jax.ShapeDtypeStruct((length, width), jnp.bfloat16)
    return pl.pallas_call(
        head_kernel,
        grid_spec=pltpu.PrefetchScalarGridSpec(
            num_scalar_prefetch=1,
            grid=(heads // block,),
            in_specs=[tile] * 4 + [pl.BlockSpec((block, length), lambda h, c: (h, 0))] + [states] * 4,
            out_specs=[tile] * 4,
        ),
        out_shape=[out] * 4,
        compiler_params=pltpu.CompilerParams(dimension_semantics=("arbitrary",)),
    )(core.astype(jnp.int32).reshape(1), *inputs, cumul_heads, *halves)


def gather_rows(row, axis):
    count = lax.axis_size(axis)
    me = lax.axis_index(axis)
    known = row[None]
    early = None
    step = 1
    while step < count:
        pairs = [(i, (i + step) % count) for i in range(count)]
        known = jnp.concatenate([known, lax.ppermute(known, axis, pairs)], 0)
        early = known if early is None else early
        step *= 2
    return known[(me - jnp.arange(count)) % count], early


def window_sum(ordered, place, first, last):
    total = jnp.zeros_like(ordered[0])
    for back in range(first, last + 1):
        index = place - back
        picked = lax.dynamic_index_in_dim(ordered, jnp.maximum(index, 0), 0, False)
        total = total + jnp.where(index >= 0, picked, jnp.zeros_like(picked))
    return total


def chip_scan(chip_totals, state, axis, chip, chips, reverse, steps):
    direction = -1 if reverse else 1
    ordered = chip_totals[::-1] if reverse else chip_totals
    place = chips - 1 - chip if reverse else chip
    sent = state
    carried = jnp.zeros_like(state)
    for count, step in enumerate(steps):
        pairs = []
        for c in range(chips):
            target = c + direction * step
            if 0 <= target < chips:
                for core in range(2):
                    pairs.append((2 * c + core, 2 * target + core))
        received = lax.ppermute(sent, axis, pairs)
        to_start = jnp.exp(window_sum(ordered, place, 1, step - 1))[:, None, None]
        carried = carried + to_start * received
        if count + 1 < len(steps):
            to_end = jnp.exp(window_sum(ordered, place, 0, step - 1))[:, None, None]
            sent = sent + to_end * received
    return carried


def shards(queries, key_vectors, values, out_grad, log_decay):
    axis = "ctx"
    total = jnp.sum(log_decay.astype(jnp.float32), axis=0)
    every_total, early = gather_rows(total, axis)
    _, queries, key_vectors, values, out_grad = lax.optimization_barrier(
        (early, queries, key_vectors, values, out_grad))
    _, state, grad_state, pieces = prepare(queries, key_vectors, values, out_grad, log_decay)
    heads = total.shape[0]
    half = heads // 2
    chips = lax.axis_size(axis) // 2
    core = lax.axis_index(axis) % 2
    partner = [(2 * c + k, 2 * c + 1 - k) for c in range(chips) for k in range(2)]

    def other_half(a):
        return lax.dynamic_slice_in_dim(a, (1 - core) * half, half, 0)

    def own_half(a):
        return lax.dynamic_slice_in_dim(a, core * half, half, 0)

    sent = (total, other_half(state), other_half(grad_state))
    other_total, other_state, other_grad = lax.ppermute(sent, axis, partner)
    first = core == 0
    mine_state = own_half(state)
    mine_grad = own_half(grad_state)
    own_total_half = own_half(total)
    other_total_half = own_half(other_total)
    one = jnp.ones_like(own_total_half)
    fwd_a = jnp.where(first, jnp.exp(other_total_half), one)[:, None, None]
    fwd_b = jnp.where(first, one, jnp.exp(own_total_half))[:, None, None]
    chip_state = fwd_a * mine_state + fwd_b * other_state
    bwd_a = jnp.where(first, one, jnp.exp(other_total_half))[:, None, None]
    bwd_b = jnp.where(first, jnp.exp(own_total_half), one)[:, None, None]
    chip_grad = bwd_a * mine_grad + bwd_b * other_grad
    chip_totals = every_total[0::2] + every_total[1::2]
    chip = lax.axis_index(axis) // 2
    steps = []
    step = 1
    while step < chips:
        steps.append(step)
        step *= 2
    turn = len(steps) // 2
    orders = (steps, steps[turn:] + steps[:turn])
    group = half // 2
    scans = []
    for chip_sum, reverse in ((chip_state, False), (chip_grad, True)):
        parts = []
        for g, order in enumerate(orders):
            group_totals = lax.dynamic_slice_in_dim(chip_totals, core * half + g * group, group, 1)
            parts.append(
                chip_scan(group_totals, chip_sum[g * group:(g + 1) * group], axis, chip, chips, reverse, order)
            )
        scans.append(jnp.concatenate(parts, 0))
    before, after = scans
    zero = jnp.zeros_like(own_total_half)
    own_decay = jnp.exp(own_total_half)
    other_decay = jnp.exp(other_total_half)

    def mix(a, x, b, y):
        return a[:, None, None] * x + b[:, None, None] * y

    keep_fwd = mix(jnp.where(first, one, other_decay), before, jnp.where(first, zero, one), other_state)
    give_fwd = mix(jnp.where(first, own_decay, one), before, jnp.where(first, one, zero), mine_state)
    keep_bwd = mix(jnp.where(first, other_decay, one), after, jnp.where(first, one, zero), other_grad)
    give_bwd = mix(jnp.where(first, one, own_decay), after, jnp.where(first, zero, one), mine_grad)
    got_fwd, got_bwd = lax.ppermute((give_fwd, give_bwd), axis, partner)
    inputs = (queries, key_vectors, values, out_grad)
    return tuple(finish(inputs, pieces, core, (keep_fwd, got_fwd, keep_bwd, got_bwd)))


def solution(mesh):
    return jax.shard_map(
        shards,
        mesh=mesh,
        in_specs=(
            P(("dp", "ctx"), None),
            P(("dp", "ctx"), None),
            P(("dp", "ctx"), None),
            P(("dp", "ctx"), None),
            P(("dp", "ctx"), None),
        ),
        out_specs=(
            P(("dp", "ctx"), None),
            P(("dp", "ctx"), None),
            P(("dp", "ctx"), None),
            P(("dp", "ctx"), None),
        ),
        check_vma=False,
    )
```

```python
import jax
import jax.numpy as jnp
from jax import lax
from jax.sharding import PartitionSpec as P
from jax.experimental import pallas as pl
from jax.experimental.pallas import tpu as pltpu

SPAN = 64


def combine(earlier, latter):
    return (earlier[0] + latter[0], jnp.exp(latter[0])[..., None, None] * earlier[1] + latter[1])


def prepare(queries, key_vectors, values, out_grad, log_decay):
    highest = lax.Precision.HIGHEST
    length = queries.shape[0]
    heads = log_decay.shape[1]
    q_rows = queries.reshape(length, heads, -1).astype(jnp.float32)
    k_rows = key_vectors.reshape(length, heads, -1).astype(jnp.float32)
    v_rows = values.reshape(length, heads, -1).astype(jnp.float32)
    g_rows = out_grad.reshape(length, heads, -1).astype(jnp.float32)
    cumul = jnp.cumsum(log_decay.astype(jnp.float32), axis=0)
    total = cumul[-1]
    query_decay = jnp.exp(cumul)
    key_decay = jnp.exp(total[None, :] - cumul)
    state = jnp.einsum("she,shf->hef", k_rows * key_decay[..., None], v_rows, precision=highest)
    grad_state = jnp.einsum("the,thf->hef", q_rows * query_decay[..., None], g_rows, precision=highest)
    pieces = jnp.transpose(cumul)
    total = jnp.sum(log_decay.astype(jnp.float32), axis=0)
    return total, state, grad_state, pieces


def split(x):
    high = x.astype(jnp.bfloat16)
    return high, (x - high.astype(jnp.float32)).astype(jnp.bfloat16)


def head_kernel(q_ref, k_ref, v_ref, g_ref, cum_ref, s_ref, gs_ref, att_ref, qg_ref, kg_ref, vg_ref):
    f32 = jnp.float32
    nn = (((1,), (0,)), ((), ()))
    nt = (((1,), (1,)), ((), ()))

    def mm(a, b, dims):
        return lax.dot_general(a, b, dims, preferred_element_type=f32)

    def mm_right(a, b, dims):
        high, low = split(b)
        return mm(a, high, dims) + mm(a, low, dims)

    def mm_left(a, b, dims):
        high, low = split(a)
        return mm(high, b, dims) + mm(low, b, dims)

    size = q_ref.shape[0]
    block = cum_ref.shape[0]
    dk = q_ref.shape[1] // block
    later = lax.broadcasted_iota(jnp.int32, (size, size), 0) >= lax.broadcasted_iota(jnp.int32, (size, size), 1)
    for j in range(block):
        cols = slice(j * dk, (j + 1) * dk)
        q = q_ref[:, cols]
        k = k_ref[:, cols]
        v = v_ref[:, cols]
        g = g_ref[:, cols]
        row = cum_ref[j:j + 1, :]
        grid_row = jnp.broadcast_to(row, (size, size))
        col = jnp.sum(jnp.where(later & (~(lax.broadcasted_iota(jnp.int32, (size, size), 0) >
                                           lax.broadcasted_iota(jnp.int32, (size, size), 1))), grid_row, 0.0),
                      axis=1, keepdims=True)
        last = row[:, size - 1:size]
        weights = jnp.where(later, jnp.exp(jnp.where(later, col - row, 0.0)), 0.0)
        scores = mm(q, k, nt) * weights
        grad_scores = mm(g, v, nt) * weights
        qd = jnp.exp(col)
        kd = jnp.exp(last - col)
        state = s_ref[j]
        grad_in = gs_ref[j]
        att_ref[:, cols] = (mm_left(scores, v, nn) + qd * mm_right(q, state, nn)).astype(att_ref.dtype)
        qg_ref[:, cols] = (mm_left(grad_scores, k, nn) + qd * mm_right(g, state, nt)).astype(qg_ref.dtype)
        kg_ref[:, cols] = (mm_left(grad_scores.T, q, nn) + kd * mm_right(v, grad_in, nt)).astype(kg_ref.dtype)
        vg_ref[:, cols] = (mm_left(scores.T, g, nn) + kd * mm_right(k, grad_in, nn)).astype(vg_ref.dtype)


def finish(inputs, cumul_heads, state_in, grad_in):
    queries = inputs[0]
    length, width = queries.shape
    heads = state_in.shape[0]
    dk = width // heads
    block = 8
    tile = pl.BlockSpec((length, block * dk), lambda h: (0, h))
    states = pl.BlockSpec((block, dk, dk), lambda h: (h, 0, 0))
    out = jax.ShapeDtypeStruct((length, width), jnp.bfloat16)
    return pl.pallas_call(
        head_kernel,
        grid=(heads // block,),
        in_specs=[tile] * 4 + [pl.BlockSpec((block, length), lambda h: (h, 0)), states, states],
        out_specs=[tile] * 4,
        out_shape=[out] * 4,
        compiler_params=pltpu.CompilerParams(dimension_semantics=("arbitrary",)),
    )(*inputs, cumul_heads, state_in, grad_in)


def gather_round(known, axis, step):
    count = lax.axis_size(axis)
    pairs = [(i, (i + step) % count) for i in range(count)]
    return jnp.concatenate([known, lax.ppermute(known, axis, pairs)], 0)


def shift_pairs(chips, step, reverse):
    direction = -1 if reverse else 1
    pairs = []
    for c in range(chips):
        target = c + direction * step
        if 0 <= target < chips:
            for core in range(2):
                pairs.append((2 * c + core, 2 * target + core))
    return pairs


def window_sum(ordered, place, first, last, own):
    total = own if first == 0 else jnp.zeros_like(own)
    for back in range(max(first, 1), last + 1):
        index = place - back
        picked = lax.dynamic_index_in_dim(ordered, jnp.maximum(index, 0), 0, False)
        total = total + jnp.where(index >= 0, picked, jnp.zeros_like(picked))
    return total


def chip_scan(chip_totals, own, state, axis, chip, chips, reverse, steps, first_received):
    ordered = chip_totals[::-1] if reverse else chip_totals
    place = chips - 1 - chip if reverse else chip
    sent = state
    carried = jnp.zeros_like(state)
    for count, step in enumerate(steps):
        if count == 0:
            received = first_received
        else:
            received = lax.ppermute(sent, axis, shift_pairs(chips, step, reverse))
        to_start = jnp.exp(window_sum(ordered, place, 1, step - 1, own))[:, None, None]
        carried = carried + to_start * received
        if count + 1 < len(steps):
            to_end = jnp.exp(window_sum(ordered, place, 0, step - 1, own))[:, None, None]
            sent = sent + to_end * received
    return carried


def shards(queries, key_vectors, values, out_grad, log_decay):
    axis = "ctx"
    total = jnp.sum(log_decay.astype(jnp.float32), axis=0)
    early = gather_round(total[None], axis, 1)
    known = gather_round(early, axis, 2)
    _, queries, key_vectors, values, out_grad = lax.optimization_barrier(
        (early, queries, key_vectors, values, out_grad))
    _, state, grad_state, pieces = prepare(queries, key_vectors, values, out_grad, log_decay)
    heads = total.shape[0]
    half = heads // 2
    chips = lax.axis_size(axis) // 2
    core = lax.axis_index(axis) % 2
    partner = [(2 * c + k, 2 * c + 1 - k) for c in range(chips) for k in range(2)]

    def other_half(a):
        return lax.dynamic_slice_in_dim(a, (1 - core) * half, half, 0)

    def own_half(a):
        return lax.dynamic_slice_in_dim(a, core * half, half, 0)

    sent = (total, other_half(state), other_half(grad_state))
    other_total, other_state, other_grad = lax.ppermute(sent, axis, partner)
    first = core == 0
    mine_state = own_half(state)
    mine_grad = own_half(grad_state)
    own_total_half = own_half(total)
    other_total_half = own_half(other_total)
    one = jnp.ones_like(own_total_half)
    fwd_a = jnp.where(first, jnp.exp(other_total_half), one)[:, None, None]
    fwd_b = jnp.where(first, one, jnp.exp(own_total_half))[:, None, None]
    chip_state = fwd_a * mine_state + fwd_b * other_state
    bwd_a = jnp.where(first, one, jnp.exp(other_total_half))[:, None, None]
    bwd_b = jnp.where(first, jnp.exp(own_total_half), one)[:, None, None]
    chip_grad = bwd_a * mine_grad + bwd_b * other_grad
    steps = []
    step = 1
    while step < chips:
        steps.append(step)
        step *= 2
    turn = len(steps) // 2
    orders = (steps, steps[turn:] + steps[:turn])
    group = half // 2
    firsts = tuple(
        lax.ppermute(chip_sum[g * group:(g + 1) * group], axis, shift_pairs(chips, order[0], reverse))
        for chip_sum, reverse in ((chip_state, False), (chip_grad, True))
        for g, order in enumerate(orders))
    known, firsts = lax.optimization_barrier((known, firsts))
    step = 4
    while step < lax.axis_size(axis):
        known = gather_round(known, axis, step)
        step *= 2
    count = lax.axis_size(axis)
    every_total = known[(lax.axis_index(axis) - jnp.arange(count)) % count]
    chip_totals = every_total[0::2] + every_total[1::2]
    chip = lax.axis_index(axis) // 2
    own_chip = own_half(total + other_total)
    scans = []
    first_index = 0
    for chip_sum, reverse in ((chip_state, False), (chip_grad, True)):
        parts = []
        for g, order in enumerate(orders):
            group_totals = lax.dynamic_slice_in_dim(chip_totals, core * half + g * group, group, 1)
            parts.append(
                chip_scan(group_totals, own_chip[g * group:(g + 1) * group], chip_sum[g * group:(g + 1) * group],
                          axis, chip, chips, reverse, order,
                          firsts[first_index])
            )
            first_index += 1
        scans.append(jnp.concatenate(parts, 0))
    before, after = scans
    total_c0 = jnp.where(first, own_total_half, other_total_half)
    total_c1 = jnp.where(first, other_total_half, own_total_half)
    state_c0 = jnp.where(first, mine_state, other_state)
    grad_c1 = jnp.where(first, other_grad, mine_grad)
    fwd_core0 = before
    fwd_core1 = jnp.exp(total_c0)[:, None, None] * before + state_c0
    bwd_core0 = jnp.exp(total_c1)[:, None, None] * after + grad_c1
    bwd_core1 = after
    keep_fwd = jnp.where(first, fwd_core0, fwd_core1)
    keep_bwd = jnp.where(first, bwd_core0, bwd_core1)
    give_fwd = jnp.where(first, fwd_core1, fwd_core0)
    give_bwd = jnp.where(first, bwd_core1, bwd_core0)
    got_fwd, got_bwd = lax.ppermute((give_fwd, give_bwd), axis, partner)

    def assemble(keep, got):
        return jnp.where(first, jnp.concatenate([keep, got], 0), jnp.concatenate([got, keep], 0))

    inputs = (queries, key_vectors, values, out_grad)
    return tuple(finish(inputs, pieces, assemble(keep_fwd, got_fwd), assemble(keep_bwd, got_bwd)))


def solution(mesh):
    return jax.shard_map(
        shards,
        mesh=mesh,
        in_specs=(
            P(("dp", "ctx"), None),
            P(("dp", "ctx"), None),
            P(("dp", "ctx"), None),
            P(("dp", "ctx"), None),
            P(("dp", "ctx"), None),
        ),
        out_specs=(
            P(("dp", "ctx"), None),
            P(("dp", "ctx"), None),
            P(("dp", "ctx"), None),
            P(("dp", "ctx"), None),
        ),
        check_vma=False,
    )
```

```python
import jax
import jax.numpy as jnp
from jax import lax
from jax.sharding import PartitionSpec as P
from jax.experimental import pallas as pl
from jax.experimental.pallas import tpu as pltpu

SPAN = 64


def combine(earlier, latter):
    return (earlier[0] + latter[0], jnp.exp(latter[0])[..., None, None] * earlier[1] + latter[1])


def prepare(queries, key_vectors, values, out_grad, log_decay):
    highest = lax.Precision.HIGHEST
    length = queries.shape[0]
    heads = log_decay.shape[1]
    q_rows = queries.reshape(length, heads, -1).astype(jnp.float32)
    k_rows = key_vectors.reshape(length, heads, -1).astype(jnp.float32)
    v_rows = values.reshape(length, heads, -1).astype(jnp.float32)
    g_rows = out_grad.reshape(length, heads, -1).astype(jnp.float32)
    cumul = jnp.cumsum(log_decay.astype(jnp.float32), axis=0)
    total = cumul[-1]
    query_decay = jnp.exp(cumul)
    key_decay = jnp.exp(total[None, :] - cumul)
    state = jnp.einsum("she,shf->hef", k_rows * key_decay[..., None], v_rows, precision=highest)
    grad_state = jnp.einsum("the,thf->hef", q_rows * query_decay[..., None], g_rows, precision=highest)
    pieces = jnp.transpose(cumul)
    total = jnp.sum(log_decay.astype(jnp.float32), axis=0)
    return total, state, grad_state, pieces


def split(x):
    high = x.astype(jnp.bfloat16)
    return high, (x - high.astype(jnp.float32)).astype(jnp.bfloat16)


def head_kernel(q_ref, k_ref, v_ref, g_ref, cum_ref, s_ref, gs_ref, att_ref, qg_ref, kg_ref, vg_ref):
    f32 = jnp.float32
    nn = (((1,), (0,)), ((), ()))
    nt = (((1,), (1,)), ((), ()))

    def mm(a, b, dims):
        return lax.dot_general(a, b, dims, preferred_element_type=f32)

    def mm_right(a, b, dims):
        high, low = split(b)
        return mm(a, high, dims) + mm(a, low, dims)

    def mm_left(a, b, dims):
        high, low = split(a)
        return mm(high, b, dims) + mm(low, b, dims)

    size = q_ref.shape[0]
    block = cum_ref.shape[0]
    dk = q_ref.shape[1] // block
    later = lax.broadcasted_iota(jnp.int32, (size, size), 0) >= lax.broadcasted_iota(jnp.int32, (size, size), 1)
    for j in range(block):
        cols = slice(j * dk, (j + 1) * dk)
        q = q_ref[:, cols]
        k = k_ref[:, cols]
        v = v_ref[:, cols]
        g = g_ref[:, cols]
        row = cum_ref[j:j + 1, :]
        grid_row = jnp.broadcast_to(row, (size, size))
        col = jnp.sum(jnp.where(later & (~(lax.broadcasted_iota(jnp.int32, (size, size), 0) >
                                           lax.broadcasted_iota(jnp.int32, (size, size), 1))), grid_row, 0.0),
                      axis=1, keepdims=True)
        last = row[:, size - 1:size]
        weights = jnp.where(later, jnp.exp(jnp.where(later, col - row, 0.0)), 0.0)
        scores = mm(q, k, nt) * weights
        grad_scores = mm(g, v, nt) * weights
        qd = jnp.exp(col)
        kd = jnp.exp(last - col)
        state = s_ref[j]
        grad_in = gs_ref[j]
        att_ref[:, cols] = (mm_left(scores, v, nn) + qd * mm_right(q, state, nn)).astype(att_ref.dtype)
        qg_ref[:, cols] = (mm_left(grad_scores, k, nn) + qd * mm_right(g, state, nt)).astype(qg_ref.dtype)
        kg_ref[:, cols] = (mm_left(grad_scores.T, q, nn) + kd * mm_right(v, grad_in, nt)).astype(kg_ref.dtype)
        vg_ref[:, cols] = (mm_left(scores.T, g, nn) + kd * mm_right(k, grad_in, nn)).astype(vg_ref.dtype)


def finish(inputs, cumul_heads, state_in, grad_in):
    queries = inputs[0]
    length, width = queries.shape
    heads = state_in.shape[0]
    dk = width // heads
    block = 8
    tile = pl.BlockSpec((length, block * dk), lambda h: (0, h))
    states = pl.BlockSpec((block, dk, dk), lambda h: (h, 0, 0))
    out = jax.ShapeDtypeStruct((length, width), jnp.bfloat16)
    return pl.pallas_call(
        head_kernel,
        grid=(heads // block,),
        in_specs=[tile] * 4 + [pl.BlockSpec((block, length), lambda h: (h, 0)), states, states],
        out_specs=[tile] * 4,
        out_shape=[out] * 4,
        compiler_params=pltpu.CompilerParams(dimension_semantics=("arbitrary",)),
    )(*inputs, cumul_heads, state_in, grad_in)


def gather_rows(row, axis):
    count = lax.axis_size(axis)
    me = lax.axis_index(axis)
    back = row[None]
    ahead = row[None]
    early = None
    step = 1
    while 2 * step <= count // 2:
        down = [(i, (i + step) % count) for i in range(count)]
        up = [(i, (i - step) % count) for i in range(count)]
        back = jnp.concatenate([back, lax.ppermute(back, axis, down)], 0)
        ahead = jnp.concatenate([ahead, lax.ppermute(ahead, axis, up)], 0)
        early = (back, ahead) if early is None else early
        step *= 2
    reach = back.shape[0]
    devices = jnp.arange(count)
    from_back = back[jnp.clip(me - devices, 0, reach - 1)]
    from_ahead = ahead[jnp.clip(devices - me, 0, reach - 1)]
    near_back = ((me - devices >= 0) & (me - devices < reach))[:, None]
    near_ahead = ((devices - me > 0) & (devices - me < reach))[:, None]
    rows = jnp.where(near_back, from_back, jnp.where(near_ahead, from_ahead, jnp.zeros_like(from_back)))
    return rows, early


def window_sum(ordered, place, first, last):
    total = jnp.zeros_like(ordered[0])
    for back in range(first, last + 1):
        index = place - back
        picked = lax.dynamic_index_in_dim(ordered, jnp.maximum(index, 0), 0, False)
        total = total + jnp.where(index >= 0, picked, jnp.zeros_like(picked))
    return total


def chip_scan(chip_totals, state, axis, chip, chips, reverse, steps):
    direction = -1 if reverse else 1
    ordered = chip_totals[::-1] if reverse else chip_totals
    place = chips - 1 - chip if reverse else chip
    sent = state
    carried = jnp.zeros_like(state)
    for count, step in enumerate(steps):
        pairs = []
        for c in range(chips):
            target = c + direction * step
            if 0 <= target < chips:
                for core in range(2):
                    pairs.append((2 * c + core, 2 * target + core))
        received = lax.ppermute(sent, axis, pairs)
        to_start = jnp.exp(window_sum(ordered, place, 1, step - 1))[:, None, None]
        carried = carried + to_start * received
        if count + 1 < len(steps):
            to_end = jnp.exp(window_sum(ordered, place, 0, step - 1))[:, None, None]
            sent = sent + to_end * received
    return carried


def shards(queries, key_vectors, values, out_grad, log_decay):
    axis = "ctx"
    total = jnp.sum(log_decay.astype(jnp.float32), axis=0)
    every_total, early = gather_rows(total, axis)
    _, queries, key_vectors, values, out_grad = lax.optimization_barrier(
        (early, queries, key_vectors, values, out_grad))
    _, state, grad_state, pieces = prepare(queries, key_vectors, values, out_grad, log_decay)
    heads = total.shape[0]
    half = heads // 2
    chips = lax.axis_size(axis) // 2
    core = lax.axis_index(axis) % 2
    partner = [(2 * c + k, 2 * c + 1 - k) for c in range(chips) for k in range(2)]

    def other_half(a):
        return lax.dynamic_slice_in_dim(a, (1 - core) * half, half, 0)

    def own_half(a):
        return lax.dynamic_slice_in_dim(a, core * half, half, 0)

    sent = (total, other_half(state), other_half(grad_state))
    other_total, other_state, other_grad = lax.ppermute(sent, axis, partner)
    first = core == 0
    mine_state = own_half(state)
    mine_grad = own_half(grad_state)
    own_total_half = own_half(total)
    other_total_half = own_half(other_total)
    one = jnp.ones_like(own_total_half)
    fwd_a = jnp.where(first, jnp.exp(other_total_half), one)[:, None, None]
    fwd_b = jnp.where(first, one, jnp.exp(own_total_half))[:, None, None]
    chip_state = fwd_a * mine_state + fwd_b * other_state
    bwd_a = jnp.where(first, one, jnp.exp(other_total_half))[:, None, None]
    bwd_b = jnp.where(first, jnp.exp(own_total_half), one)[:, None, None]
    chip_grad = bwd_a * mine_grad + bwd_b * other_grad
    chip_totals = every_total[0::2] + every_total[1::2]
    chip = lax.axis_index(axis) // 2
    steps = []
    step = 1
    while step < chips:
        steps.append(step)
        step *= 2
    turn = len(steps) // 2
    orders = (steps, steps[turn:] + steps[:turn])
    group = half // 2
    scans = []
    for chip_sum, reverse in ((chip_state, False), (chip_grad, True)):
        parts = []
        for g, order in enumerate(orders):
            group_totals = lax.dynamic_slice_in_dim(chip_totals, core * half + g * group, group, 1)
            parts.append(
                chip_scan(group_totals, chip_sum[g * group:(g + 1) * group], axis, chip, chips, reverse, order)
            )
        scans.append(jnp.concatenate(parts, 0))
    before, after = scans
    total_c0 = jnp.where(first, own_total_half, other_total_half)
    total_c1 = jnp.where(first, other_total_half, own_total_half)
    state_c0 = jnp.where(first, mine_state, other_state)
    grad_c1 = jnp.where(first, other_grad, mine_grad)
    fwd_core0 = before
    fwd_core1 = jnp.exp(total_c0)[:, None, None] * before + state_c0
    bwd_core0 = jnp.exp(total_c1)[:, None, None] * after + grad_c1
    bwd_core1 = after
    keep_fwd = jnp.where(first, fwd_core0, fwd_core1)
    keep_bwd = jnp.where(first, bwd_core0, bwd_core1)
    give_fwd = jnp.where(first, fwd_core1, fwd_core0)
    give_bwd = jnp.where(first, bwd_core1, bwd_core0)
    got_fwd, got_bwd = lax.ppermute((give_fwd, give_bwd), axis, partner)

    def assemble(keep, got):
        return jnp.where(first, jnp.concatenate([keep, got], 0), jnp.concatenate([got, keep], 0))

    inputs = (queries, key_vectors, values, out_grad)
    return tuple(finish(inputs, pieces, assemble(keep_fwd, got_fwd), assemble(keep_bwd, got_bwd)))


def solution(mesh):
    return jax.shard_map(
        shards,
        mesh=mesh,
        in_specs=(
            P(("dp", "ctx"), None),
            P(("dp", "ctx"), None),
            P(("dp", "ctx"), None),
            P(("dp", "ctx"), None),
            P(("dp", "ctx"), None),
        ),
        out_specs=(
            P(("dp", "ctx"), None),
            P(("dp", "ctx"), None),
            P(("dp", "ctx"), None),
            P(("dp", "ctx"), None),
        ),
        check_vma=False,
    )
```

```python
import jax
import jax.numpy as jnp
from jax import lax
from jax.sharding import PartitionSpec as P
from jax.experimental import pallas as pl
from jax.experimental.pallas import tpu as pltpu

SPAN = 64


def combine(earlier, latter):
    return (earlier[0] + latter[0], jnp.exp(latter[0])[..., None, None] * earlier[1] + latter[1])


def prepare(queries, key_vectors, values, out_grad, log_decay):
    highest = lax.Precision.HIGHEST
    length = queries.shape[0]
    heads = log_decay.shape[1]
    q_rows = queries.reshape(length, heads, -1).astype(jnp.float32)
    k_rows = key_vectors.reshape(length, heads, -1).astype(jnp.float32)
    v_rows = values.reshape(length, heads, -1).astype(jnp.float32)
    g_rows = out_grad.reshape(length, heads, -1).astype(jnp.float32)
    cumul = jnp.cumsum(log_decay.astype(jnp.float32), axis=0)
    total = cumul[-1]
    query_decay = jnp.exp(cumul)
    key_decay = jnp.exp(total[None, :] - cumul)
    state = jnp.einsum("she,shf->hef", k_rows * key_decay[..., None], v_rows, precision=highest)
    grad_state = jnp.einsum("the,thf->hef", q_rows * query_decay[..., None], g_rows, precision=highest)
    pieces = jnp.transpose(cumul)
    total = jnp.sum(log_decay.astype(jnp.float32), axis=0)
    return total, state, grad_state, pieces


def split(x):
    high = x.astype(jnp.bfloat16)
    return high, (x - high.astype(jnp.float32)).astype(jnp.bfloat16)


def head_kernel(q_ref, k_ref, v_ref, g_ref, cum_ref, s_ref, gs_ref, att_ref, qg_ref, kg_ref, vg_ref):
    f32 = jnp.float32
    nn = (((1,), (0,)), ((), ()))
    nt = (((1,), (1,)), ((), ()))

    def mm(a, b, dims):
        return lax.dot_general(a, b, dims, preferred_element_type=f32)

    def mm_right(a, b, dims):
        high, low = split(b)
        return mm(a, high, dims) + mm(a, low, dims)

    def mm_left(a, b, dims):
        high, low = split(a)
        return mm(high, b, dims) + mm(low, b, dims)

    size = q_ref.shape[0]
    block = cum_ref.shape[0]
    dk = q_ref.shape[1] // block
    later = lax.broadcasted_iota(jnp.int32, (size, size), 0) >= lax.broadcasted_iota(jnp.int32, (size, size), 1)
    columns = cum_ref[...].T
    for j in range(block):
        cols = slice(j * dk, (j + 1) * dk)
        q = q_ref[:, cols]
        k = k_ref[:, cols]
        v = v_ref[:, cols]
        g = g_ref[:, cols]
        row = cum_ref[j:j + 1, :]
        col = columns[:, j:j + 1]
        last = row[:, size - 1:size]
        weights = jnp.where(later, jnp.exp(jnp.where(later, col - row, 0.0)), 0.0)
        scores = mm(q, k, nt) * weights
        grad_scores = mm(g, v, nt) * weights
        qd = jnp.exp(col)
        kd = jnp.exp(last - col)
        state_high, state_low = split(s_ref[j])
        grad_high, grad_low = split(gs_ref[j])

        def carried(a, high, low, dims):
            return mm(a, high, dims) + mm(a, low, dims)

        att_ref[:, cols] = (mm_left(scores, v, nn) + qd * carried(q, state_high, state_low, nn)).astype(att_ref.dtype)
        qg_ref[:, cols] = (mm_left(grad_scores, k, nn) + qd * carried(g, state_high, state_low, nt)).astype(qg_ref.dtype)
        kg_ref[:, cols] = (mm_left(grad_scores.T, q, nn) + kd * carried(v, grad_high, grad_low, nt)).astype(kg_ref.dtype)
        vg_ref[:, cols] = (mm_left(scores.T, g, nn) + kd * carried(k, grad_high, grad_low, nn)).astype(vg_ref.dtype)


def finish(inputs, cumul_heads, state_in, grad_in):
    queries = inputs[0]
    length, width = queries.shape
    heads = state_in.shape[0]
    dk = width // heads
    block = 8
    tile = pl.BlockSpec((length, block * dk), lambda h: (0, h))
    states = pl.BlockSpec((block, dk, dk), lambda h: (h, 0, 0))
    out = jax.ShapeDtypeStruct((length, width), jnp.bfloat16)
    return pl.pallas_call(
        head_kernel,
        grid=(heads // block,),
        in_specs=[tile] * 4 + [pl.BlockSpec((block, length), lambda h: (h, 0)), states, states],
        out_specs=[tile] * 4,
        out_shape=[out] * 4,
        compiler_params=pltpu.CompilerParams(dimension_semantics=("arbitrary",)),
    )(*inputs, cumul_heads, state_in, grad_in)


def gather_rows(row, axis):
    count = lax.axis_size(axis)
    me = lax.axis_index(axis)
    known = row[None]
    early = None
    step = 1
    while step < count:
        pairs = [(i, (i + step) % count) for i in range(count)]
        known = jnp.concatenate([known, lax.ppermute(known, axis, pairs)], 0)
        early = known if early is None else early
        step *= 2
    return known[(me - jnp.arange(count)) % count], early


def window_sum(ordered, place, first, last):
    total = jnp.zeros_like(ordered[0])
    for back in range(first, last + 1):
        index = place - back
        picked = lax.dynamic_index_in_dim(ordered, jnp.maximum(index, 0), 0, False)
        total = total + jnp.where(index >= 0, picked, jnp.zeros_like(picked))
    return total


def chip_scan(chip_totals, state, axis, chip, chips, reverse, steps):
    direction = -1 if reverse else 1
    ordered = chip_totals[::-1] if reverse else chip_totals
    place = chips - 1 - chip if reverse else chip
    sent = state
    carried = jnp.zeros_like(state)
    for count, step in enumerate(steps):
        pairs = []
        for c in range(chips):
            target = c + direction * step
            if 0 <= target < chips:
                for core in range(2):
                    pairs.append((2 * c + core, 2 * target + core))
        received = lax.ppermute(sent, axis, pairs)
        to_start = jnp.exp(window_sum(ordered, place, 1, step - 1))[:, None, None]
        carried = carried + to_start * received
        if count + 1 < len(steps):
            to_end = jnp.exp(window_sum(ordered, place, 0, step - 1))[:, None, None]
            sent = sent + to_end * received
    return carried


def shards(queries, key_vectors, values, out_grad, log_decay):
    axis = "ctx"
    total = jnp.sum(log_decay.astype(jnp.float32), axis=0)
    every_total, early = gather_rows(total, axis)
    _, queries, key_vectors, values, out_grad = lax.optimization_barrier(
        (early, queries, key_vectors, values, out_grad))
    _, state, grad_state, pieces = prepare(queries, key_vectors, values, out_grad, log_decay)
    heads = total.shape[0]
    half = heads // 2
    chips = lax.axis_size(axis) // 2
    core = lax.axis_index(axis) % 2
    partner = [(2 * c + k, 2 * c + 1 - k) for c in range(chips) for k in range(2)]

    def other_half(a):
        return lax.dynamic_slice_in_dim(a, (1 - core) * half, half, 0)

    def own_half(a):
        return lax.dynamic_slice_in_dim(a, core * half, half, 0)

    sent = (total, other_half(state), other_half(grad_state))
    other_total, other_state, other_grad = lax.ppermute(sent, axis, partner)
    first = core == 0
    mine_state = own_half(state)
    mine_grad = own_half(grad_state)
    own_total_half = own_half(total)
    other_total_half = own_half(other_total)
    one = jnp.ones_like(own_total_half)
    fwd_a = jnp.where(first, jnp.exp(other_total_half), one)[:, None, None]
    fwd_b = jnp.where(first, one, jnp.exp(own_total_half))[:, None, None]
    chip_state = fwd_a * mine_state + fwd_b * other_state
    bwd_a = jnp.where(first, one, jnp.exp(other_total_half))[:, None, None]
    bwd_b = jnp.where(first, jnp.exp(own_total_half), one)[:, None, None]
    chip_grad = bwd_a * mine_grad + bwd_b * other_grad
    chip_totals = every_total[0::2] + every_total[1::2]
    chip = lax.axis_index(axis) // 2
    steps = []
    step = 1
    while step < chips:
        steps.append(step)
        step *= 2
    turn = len(steps) // 2
    orders = (steps, steps[turn:] + steps[:turn])
    group = half // 2
    scans = []
    for chip_sum, reverse in ((chip_state, False), (chip_grad, True)):
        parts = []
        for g, order in enumerate(orders):
            group_totals = lax.dynamic_slice_in_dim(chip_totals, core * half + g * group, group, 1)
            parts.append(
                chip_scan(group_totals, chip_sum[g * group:(g + 1) * group], axis, chip, chips, reverse, order)
            )
        scans.append(jnp.concatenate(parts, 0))
    before, after = scans
    total_c0 = jnp.where(first, own_total_half, other_total_half)
    total_c1 = jnp.where(first, other_total_half, own_total_half)
    state_c0 = jnp.where(first, mine_state, other_state)
    grad_c1 = jnp.where(first, other_grad, mine_grad)
    fwd_core0 = before
    fwd_core1 = jnp.exp(total_c0)[:, None, None] * before + state_c0
    bwd_core0 = jnp.exp(total_c1)[:, None, None] * after + grad_c1
    bwd_core1 = after
    keep_fwd = jnp.where(first, fwd_core0, fwd_core1)
    keep_bwd = jnp.where(first, bwd_core0, bwd_core1)
    give_fwd = jnp.where(first, fwd_core1, fwd_core0)
    give_bwd = jnp.where(first, bwd_core1, bwd_core0)
    got_fwd, got_bwd = lax.ppermute((give_fwd, give_bwd), axis, partner)

    def assemble(keep, got):
        return jnp.where(first, jnp.concatenate([keep, got], 0), jnp.concatenate([got, keep], 0))

    inputs = (queries, key_vectors, values, out_grad)
    return tuple(finish(inputs, pieces, assemble(keep_fwd, got_fwd), assemble(keep_bwd, got_bwd)))


def solution(mesh):
    return jax.shard_map(
        shards,
        mesh=mesh,
        in_specs=(
            P(("dp", "ctx"), None),
            P(("dp", "ctx"), None),
            P(("dp", "ctx"), None),
            P(("dp", "ctx"), None),
            P(("dp", "ctx"), None),
        ),
        out_specs=(
            P(("dp", "ctx"), None),
            P(("dp", "ctx"), None),
            P(("dp", "ctx"), None),
            P(("dp", "ctx"), None),
        ),
        check_vma=False,
    )
```

```python
import jax
import jax.numpy as jnp
from jax import lax
from jax.sharding import PartitionSpec as P
from jax.experimental import pallas as pl
from jax.experimental.pallas import tpu as pltpu

SPAN = 64


def combine(earlier, latter):
    return (earlier[0] + latter[0], jnp.exp(latter[0])[..., None, None] * earlier[1] + latter[1])


def prepare(queries, key_vectors, values, out_grad, log_decay):
    highest = lax.Precision.HIGHEST
    length = queries.shape[0]
    heads = log_decay.shape[1]
    q_rows = queries.reshape(length, heads, -1).astype(jnp.float32)
    k_rows = key_vectors.reshape(length, heads, -1).astype(jnp.float32)
    v_rows = values.reshape(length, heads, -1).astype(jnp.float32)
    g_rows = out_grad.reshape(length, heads, -1).astype(jnp.float32)
    cumul = jnp.cumsum(log_decay.astype(jnp.float32), axis=0)
    total = cumul[-1]
    query_decay = jnp.exp(cumul)
    key_decay = jnp.exp(total[None, :] - cumul)
    state = jnp.einsum("she,shf->hef", k_rows * key_decay[..., None], v_rows, precision=highest)
    grad_state = jnp.einsum("the,thf->hef", q_rows * query_decay[..., None], g_rows, precision=highest)
    pieces = jnp.transpose(cumul)
    total = jnp.sum(log_decay.astype(jnp.float32), axis=0)
    return total, state, grad_state, pieces


def split(x):
    high = x.astype(jnp.bfloat16)
    return high, (x - high.astype(jnp.float32)).astype(jnp.bfloat16)


def head_kernel(core_ref, q_ref, k_ref, v_ref, g_ref, cum_ref, keep_ref, got_ref, keep_g_ref, got_g_ref,
                att_ref, qg_ref, kg_ref, vg_ref):
    f32 = jnp.float32
    nn = (((1,), (0,)), ((), ()))
    nt = (((1,), (1,)), ((), ()))

    def mm(a, b, dims):
        return lax.dot_general(a, b, dims, preferred_element_type=f32)

    def mm_right(a, b, dims):
        high, low = split(b)
        return mm(a, high, dims) + mm(a, low, dims)

    def mm_left(a, b, dims):
        high, low = split(a)
        return mm(high, b, dims) + mm(low, b, dims)

    size = q_ref.shape[0]
    block = cum_ref.shape[0]
    dk = q_ref.shape[1] // block
    later = lax.broadcasted_iota(jnp.int32, (size, size), 0) >= lax.broadcasted_iota(jnp.int32, (size, size), 1)
    kept = pl.program_id(0) // 2 == core_ref[0]
    for j in range(block):
        cols = slice(j * dk, (j + 1) * dk)
        q = q_ref[:, cols]
        k = k_ref[:, cols]
        v = v_ref[:, cols]
        g = g_ref[:, cols]
        row = cum_ref[j:j + 1, :]
        grid_row = jnp.broadcast_to(row, (size, size))
        col = jnp.sum(jnp.where(later & (~(lax.broadcasted_iota(jnp.int32, (size, size), 0) >
                                           lax.broadcasted_iota(jnp.int32, (size, size), 1))), grid_row, 0.0),
                      axis=1, keepdims=True)
        last = row[:, size - 1:size]
        weights = jnp.where(later, jnp.exp(jnp.where(later, col - row, 0.0)), 0.0)
        scores = mm(q, k, nt) * weights
        grad_scores = mm(g, v, nt) * weights
        qd = jnp.exp(col)
        kd = jnp.exp(last - col)
        state = jnp.where(kept, keep_ref[j], got_ref[j])
        grad_in = jnp.where(kept, keep_g_ref[j], got_g_ref[j])
        att_ref[:, cols] = (mm_left(scores, v, nn) + qd * mm_right(q, state, nn)).astype(att_ref.dtype)
        qg_ref[:, cols] = (mm_left(grad_scores, k, nn) + qd * mm_right(g, state, nt)).astype(qg_ref.dtype)
        kg_ref[:, cols] = (mm_left(grad_scores.T, q, nn) + kd * mm_right(v, grad_in, nt)).astype(kg_ref.dtype)
        vg_ref[:, cols] = (mm_left(scores.T, g, nn) + kd * mm_right(k, grad_in, nn)).astype(vg_ref.dtype)


def finish(inputs, cumul_heads, core, halves):
    queries = inputs[0]
    length, width = queries.shape
    half = halves[0].shape[0]
    heads = 2 * half
    dk = width // heads
    block = 8
    steps = half // block
    tile = pl.BlockSpec((length, block * dk), lambda h, c: (0, h))
    states = pl.BlockSpec((block, dk, dk), lambda h, c: (h % steps, 0, 0))
    out = jax.ShapeDtypeStruct((length, width), jnp.bfloat16)
    return pl.pallas_call(
        head_kernel,
        grid_spec=pltpu.PrefetchScalarGridSpec(
            num_scalar_prefetch=1,
            grid=(heads // block,),
            in_specs=[tile] * 4 + [pl.BlockSpec((block, length), lambda h, c: (h, 0))] + [states] * 4,
            out_specs=[tile] * 4,
        ),
        out_shape=[out] * 4,
        compiler_params=pltpu.CompilerParams(dimension_semantics=("arbitrary",)),
    )(core.astype(jnp.int32).reshape(1), *inputs, cumul_heads, *halves)


def gather_rows(row, axis):
    count = lax.axis_size(axis)
    me = lax.axis_index(axis)
    known = row[None]
    early = None
    step = 1
    while step < count:
        pairs = [(i, (i + step) % count) for i in range(count)]
        known = jnp.concatenate([known, lax.ppermute(known, axis, pairs)], 0)
        early = known if early is None else early
        step *= 2
    return known[(me - jnp.arange(count)) % count], early


def window_sum(ordered, place, first, last):
    total = jnp.zeros_like(ordered[0])
    for back in range(first, last + 1):
        index = place - back
        picked = lax.dynamic_index_in_dim(ordered, jnp.maximum(index, 0), 0, False)
        total = total + jnp.where(index >= 0, picked, jnp.zeros_like(picked))
    return total


def chip_scan(chip_totals, state, axis, chip, chips, reverse, steps):
    direction = -1 if reverse else 1
    ordered = chip_totals[::-1] if reverse else chip_totals
    place = chips - 1 - chip if reverse else chip
    sent = state
    carried = jnp.zeros_like(state)
    for count, step in enumerate(steps):
        pairs = []
        for c in range(chips):
            target = c + direction * step
            if 0 <= target < chips:
                for core in range(2):
                    pairs.append((2 * c + core, 2 * target + core))
        received = lax.ppermute(sent, axis, pairs)
        to_start = jnp.exp(window_sum(ordered, place, 1, step - 1))[:, None, None]
        carried = carried + to_start * received
        if count + 1 < len(steps):
            to_end = jnp.exp(window_sum(ordered, place, 0, step - 1))[:, None, None]
            sent = sent + to_end * received
    return carried


def shards(queries, key_vectors, values, out_grad, log_decay):
    axis = "ctx"
    total = jnp.sum(log_decay.astype(jnp.float32), axis=0)
    every_total, early = gather_rows(total, axis)
    _, queries, key_vectors, values, out_grad = lax.optimization_barrier(
        (early, queries, key_vectors, values, out_grad))
    _, state, grad_state, pieces = prepare(queries, key_vectors, values, out_grad, log_decay)
    heads = total.shape[0]
    half = heads // 2
    chips = lax.axis_size(axis) // 2
    core = lax.axis_index(axis) % 2
    partner = [(2 * c + k, 2 * c + 1 - k) for c in range(chips) for k in range(2)]

    def other_half(a):
        return lax.dynamic_slice_in_dim(a, (1 - core) * half, half, 0)

    def own_half(a):
        return lax.dynamic_slice_in_dim(a, core * half, half, 0)

    sent = (total, other_half(state), other_half(grad_state))
    other_total, other_state, other_grad = lax.ppermute(sent, axis, partner)
    first = core == 0
    mine_state = own_half(state)
    mine_grad = own_half(grad_state)
    own_total_half = own_half(total)
    other_total_half = own_half(other_total)
    one = jnp.ones_like(own_total_half)
    fwd_a = jnp.where(first, jnp.exp(other_total_half), one)[:, None, None]
    fwd_b = jnp.where(first, one, jnp.exp(own_total_half))[:, None, None]
    chip_state = fwd_a * mine_state + fwd_b * other_state
    bwd_a = jnp.where(first, one, jnp.exp(other_total_half))[:, None, None]
    bwd_b = jnp.where(first, jnp.exp(own_total_half), one)[:, None, None]
    chip_grad = bwd_a * mine_grad + bwd_b * other_grad
    chip_totals = every_total[0::2] + every_total[1::2]
    chip = lax.axis_index(axis) // 2
    steps = []
    step = 1
    while step < chips:
        steps.append(step)
        step *= 2
    turn = len(steps) // 2
    orders = (steps, steps[turn:] + steps[:turn])
    group = half // 2
    scans = []
    for chip_sum, reverse in ((chip_state, False), (chip_grad, True)):
        parts = []
        for g, order in enumerate(orders):
            group_totals = lax.dynamic_slice_in_dim(chip_totals, core * half + g * group, group, 1)
            parts.append(
                chip_scan(group_totals, chip_sum[g * group:(g + 1) * group], axis, chip, chips, reverse, order)
            )
        scans.append(jnp.concatenate(parts, 0))
    before, after = scans
    total_c0 = jnp.where(first, own_total_half, other_total_half)
    total_c1 = jnp.where(first, other_total_half, own_total_half)
    state_c0 = jnp.where(first, mine_state, other_state)
    grad_c1 = jnp.where(first, other_grad, mine_grad)
    fwd_core0 = before
    fwd_core1 = jnp.exp(total_c0)[:, None, None] * before + state_c0
    bwd_core0 = jnp.exp(total_c1)[:, None, None] * after + grad_c1
    bwd_core1 = after
    keep_fwd = jnp.where(first, fwd_core0, fwd_core1)
    keep_bwd = jnp.where(first, bwd_core0, bwd_core1)
    give_fwd = jnp.where(first, fwd_core1, fwd_core0)
    give_bwd = jnp.where(first, bwd_core1, bwd_core0)
    got_fwd, got_bwd = lax.ppermute((give_fwd, give_bwd), axis, partner)

    inputs = (queries, key_vectors, values, out_grad)
    return tuple(finish(inputs, pieces, core, (keep_fwd, got_fwd, keep_bwd, got_bwd)))


def solution(mesh):
    return jax.shard_map(
        shards,
        mesh=mesh,
        in_specs=(
            P(("dp", "ctx"), None),
            P(("dp", "ctx"), None),
            P(("dp", "ctx"), None),
            P(("dp", "ctx"), None),
            P(("dp", "ctx"), None),
        ),
        out_specs=(
            P(("dp", "ctx"), None),
            P(("dp", "ctx"), None),
            P(("dp", "ctx"), None),
            P(("dp", "ctx"), None),
        ),
        check_vma=False,
    )
```

```python
import jax
import jax.numpy as jnp
from jax import lax
from jax.sharding import PartitionSpec as P
from jax.experimental import pallas as pl
from jax.experimental.pallas import tpu as pltpu

SPAN = 64


def combine(earlier, latter):
    return (earlier[0] + latter[0], jnp.exp(latter[0])[..., None, None] * earlier[1] + latter[1])


def prepare(queries, key_vectors, values, out_grad, log_decay):
    highest = lax.Precision.HIGHEST
    length = queries.shape[0]
    heads = log_decay.shape[1]
    q_rows = queries.reshape(length, heads, -1).astype(jnp.float32)
    k_rows = key_vectors.reshape(length, heads, -1).astype(jnp.float32)
    v_rows = values.reshape(length, heads, -1).astype(jnp.float32)
    g_rows = out_grad.reshape(length, heads, -1).astype(jnp.float32)
    cumul = jnp.cumsum(log_decay.astype(jnp.float32), axis=0)
    total = cumul[-1]
    query_decay = jnp.exp(cumul)
    key_decay = jnp.exp(total[None, :] - cumul)
    state = jnp.einsum("she,shf->hef", k_rows * key_decay[..., None], v_rows, precision=highest)
    grad_state = jnp.einsum("the,thf->hef", q_rows * query_decay[..., None], g_rows, precision=highest)
    pieces = jnp.transpose(cumul)
    total = jnp.sum(log_decay.astype(jnp.float32), axis=0)
    return total, state, grad_state, pieces


def split(x):
    high = x.astype(jnp.bfloat16)
    return high, (x - high.astype(jnp.float32)).astype(jnp.bfloat16)


def head_kernel(core_ref, q_ref, k_ref, v_ref, g_ref, cum_ref, keep_ref, got_ref, keep_g_ref, got_g_ref,
                att_ref, qg_ref, kg_ref, vg_ref):
    f32 = jnp.float32
    nn = (((1,), (0,)), ((), ()))
    nt = (((1,), (1,)), ((), ()))

    def mm(a, b, dims):
        return lax.dot_general(a, b, dims, preferred_element_type=f32)

    def mm_right(a, b, dims):
        high, low = split(b)
        return mm(a, high, dims) + mm(a, low, dims)

    def mm_left(a, b, dims):
        high, low = split(a)
        return mm(high, b, dims) + mm(low, b, dims)

    size = q_ref.shape[0]
    block = cum_ref.shape[0]
    dk = q_ref.shape[1] // block
    later = lax.broadcasted_iota(jnp.int32, (size, size), 0) >= lax.broadcasted_iota(jnp.int32, (size, size), 1)
    kept = pl.program_id(0) // (keep_ref.shape[0] // block) == core_ref[0]
    for j in range(block):
        cols = slice(j * dk, (j + 1) * dk)
        q = q_ref[:, cols]
        k = k_ref[:, cols]
        v = v_ref[:, cols]
        g = g_ref[:, cols]
        row = cum_ref[j:j + 1, :]
        grid_row = jnp.broadcast_to(row, (size, size))
        col = jnp.sum(jnp.where(later & (~(lax.broadcasted_iota(jnp.int32, (size, size), 0) >
                                           lax.broadcasted_iota(jnp.int32, (size, size), 1))), grid_row, 0.0),
                      axis=1, keepdims=True)
        last = row[:, size - 1:size]
        weights = jnp.where(later, jnp.exp(jnp.where(later, col - row, 0.0)), 0.0)
        scores = mm(q, k, nt) * weights
        grad_scores = mm(g, v, nt) * weights
        qd = jnp.exp(col)
        kd = jnp.exp(last - col)
        state = jnp.where(kept, keep_ref[j], got_ref[j])
        grad_in = jnp.where(kept, keep_g_ref[j], got_g_ref[j])
        att_ref[:, cols] = (mm_left(scores, v, nn) + qd * mm_right(q, state, nn)).astype(att_ref.dtype)
        qg_ref[:, cols] = (mm_left(grad_scores, k, nn) + qd * mm_right(g, state, nt)).astype(qg_ref.dtype)
        kg_ref[:, cols] = (mm_left(grad_scores.T, q, nn) + kd * mm_right(v, grad_in, nt)).astype(kg_ref.dtype)
        vg_ref[:, cols] = (mm_left(scores.T, g, nn) + kd * mm_right(k, grad_in, nn)).astype(vg_ref.dtype)


def finish(inputs, cumul_heads, core, halves):
    queries = inputs[0]
    length, width = queries.shape
    half = halves[0].shape[0]
    heads = 2 * half
    dk = width // heads
    block = 16
    steps = half // block
    tile = pl.BlockSpec((length, block * dk), lambda h, c: (0, h))
    states = pl.BlockSpec((block, dk, dk), lambda h, c: (h % steps, 0, 0))
    out = jax.ShapeDtypeStruct((length, width), jnp.bfloat16)
    return pl.pallas_call(
        head_kernel,
        grid_spec=pltpu.PrefetchScalarGridSpec(
            num_scalar_prefetch=1,
            grid=(heads // block,),
            in_specs=[tile] * 4 + [pl.BlockSpec((block, length), lambda h, c: (h, 0))] + [states] * 4,
            out_specs=[tile] * 4,
        ),
        out_shape=[out] * 4,
        compiler_params=pltpu.CompilerParams(dimension_semantics=("arbitrary",)),
    )(core.astype(jnp.int32).reshape(1), *inputs, cumul_heads, *halves)


def gather_rows(row, axis):
    count = lax.axis_size(axis)
    me = lax.axis_index(axis)
    known = row[None]
    early = None
    step = 1
    while step < count:
        pairs = [(i, (i + step) % count) for i in range(count)]
        known = jnp.concatenate([known, lax.ppermute(known, axis, pairs)], 0)
        early = known if early is None else early
        step *= 2
    return known[(me - jnp.arange(count)) % count], early


def window_sum(ordered, place, first, last):
    total = jnp.zeros_like(ordered[0])
    for back in range(first, last + 1):
        index = place - back
        picked = lax.dynamic_index_in_dim(ordered, jnp.maximum(index, 0), 0, False)
        total = total + jnp.where(index >= 0, picked, jnp.zeros_like(picked))
    return total


def chip_scan(chip_totals, state, axis, chip, chips, reverse, steps):
    direction = -1 if reverse else 1
    ordered = chip_totals[::-1] if reverse else chip_totals
    place = chips - 1 - chip if reverse else chip
    sent = state
    carried = jnp.zeros_like(state)
    for count, step in enumerate(steps):
        pairs = []
        for c in range(chips):
            target = c + direction * step
            if 0 <= target < chips:
                for core in range(2):
                    pairs.append((2 * c + core, 2 * target + core))
        received = lax.ppermute(sent, axis, pairs)
        to_start = jnp.exp(window_sum(ordered, place, 1, step - 1))[:, None, None]
        carried = carried + to_start * received
        if count + 1 < len(steps):
            to_end = jnp.exp(window_sum(ordered, place, 0, step - 1))[:, None, None]
            sent = sent + to_end * received
    return carried


def shards(queries, key_vectors, values, out_grad, log_decay):
    axis = "ctx"
    total = jnp.sum(log_decay.astype(jnp.float32), axis=0)
    every_total, early = gather_rows(total, axis)
    _, queries, key_vectors, values, out_grad = lax.optimization_barrier(
        (early, queries, key_vectors, values, out_grad))
    _, state, grad_state, pieces = prepare(queries, key_vectors, values, out_grad, log_decay)
    heads = total.shape[0]
    half = heads // 2
    chips = lax.axis_size(axis) // 2
    core = lax.axis_index(axis) % 2
    partner = [(2 * c + k, 2 * c + 1 - k) for c in range(chips) for k in range(2)]

    def other_half(a):
        return lax.dynamic_slice_in_dim(a, (1 - core) * half, half, 0)

    def own_half(a):
        return lax.dynamic_slice_in_dim(a, core * half, half, 0)

    sent = (total, other_half(state), other_half(grad_state))
    other_total, other_state, other_grad = lax.ppermute(sent, axis, partner)
    first = core == 0
    mine_state = own_half(state)
    mine_grad = own_half(grad_state)
    own_total_half = own_half(total)
    other_total_half = own_half(other_total)
    one = jnp.ones_like(own_total_half)
    fwd_a = jnp.where(first, jnp.exp(other_total_half), one)[:, None, None]
    fwd_b = jnp.where(first, one, jnp.exp(own_total_half))[:, None, None]
    chip_state = fwd_a * mine_state + fwd_b * other_state
    bwd_a = jnp.where(first, one, jnp.exp(other_total_half))[:, None, None]
    bwd_b = jnp.where(first, jnp.exp(own_total_half), one)[:, None, None]
    chip_grad = bwd_a * mine_grad + bwd_b * other_grad
    chip_totals = every_total[0::2] + every_total[1::2]
    chip = lax.axis_index(axis) // 2
    steps = []
    step = 1
    while step < chips:
        steps.append(step)
        step *= 2
    turn = len(steps) // 2
    orders = (steps, steps[turn:] + steps[:turn])
    group = half // 2
    scans = []
    for chip_sum, reverse in ((chip_state, False), (chip_grad, True)):
        parts = []
        for g, order in enumerate(orders):
            group_totals = lax.dynamic_slice_in_dim(chip_totals, core * half + g * group, group, 1)
            parts.append(
                chip_scan(group_totals, chip_sum[g * group:(g + 1) * group], axis, chip, chips, reverse, order)
            )
        scans.append(jnp.concatenate(parts, 0))
    before, after = scans
    total_c0 = jnp.where(first, own_total_half, other_total_half)
    total_c1 = jnp.where(first, other_total_half, own_total_half)
    state_c0 = jnp.where(first, mine_state, other_state)
    grad_c1 = jnp.where(first, other_grad, mine_grad)
    fwd_core0 = before
    fwd_core1 = jnp.exp(total_c0)[:, None, None] * before + state_c0
    bwd_core0 = jnp.exp(total_c1)[:, None, None] * after + grad_c1
    bwd_core1 = after
    keep_fwd = jnp.where(first, fwd_core0, fwd_core1)
    keep_bwd = jnp.where(first, bwd_core0, bwd_core1)
    give_fwd = jnp.where(first, fwd_core1, fwd_core0)
    give_bwd = jnp.where(first, bwd_core1, bwd_core0)
    got_fwd, got_bwd = lax.ppermute((give_fwd, give_bwd), axis, partner)

    inputs = (queries, key_vectors, values, out_grad)
    return tuple(finish(inputs, pieces, core, (keep_fwd, got_fwd, keep_bwd, got_bwd)))


def solution(mesh):
    return jax.shard_map(
        shards,
        mesh=mesh,
        in_specs=(
            P(("dp", "ctx"), None),
            P(("dp", "ctx"), None),
            P(("dp", "ctx"), None),
            P(("dp", "ctx"), None),
            P(("dp", "ctx"), None),
        ),
        out_specs=(
            P(("dp", "ctx"), None),
            P(("dp", "ctx"), None),
            P(("dp", "ctx"), None),
            P(("dp", "ctx"), None),
        ),
        check_vma=False,
    )
```
